128 devices in a mesh: req: 16 (over y, x), kvh: 8 (over z, core).
Axes of the slice: x: 4, y: 4, z: 4, core: 2. Of those that a mesh axis runs over, the one named last changes fastest.
Arguments:
- states: bfloat16 [128, 2560], P('req', 'kvh'), may hold values from -6 to 6
- attn_gain: bfloat16 [2560], replicated, may hold values from 0.099609375 to 1.8984375
- w_query: bfloat16 [2560, 4096], P(None, 'kvh'), may hold values from -0.125 to 0.125
- w_key: bfloat16 [2560, 1024], P(None, 'kvh'), may hold values from -0.125 to 0.125
- w_value: bfloat16 [2560, 1024], P(None, 'kvh'), may hold values from -0.125 to 0.125
- query_gain: bfloat16 [128], replicated, may hold values from 0.5 to 2
- key_gain: bfloat16 [128], replicated, may hold values from 0.5 to 2
- w_output: bfloat16 [4096, 2560], P('kvh'), may hold values from -0.25 to 0.25
- ffn_gain: bfloat16 [2560], P('kvh'), may hold values from 0.099609375 to 1.8984375
- w_gate: bfloat16 [2560, 9728], P('kvh', 'req'), may hold values from -0.125 to 0.125
- w_up: bfloat16 [2560, 9728], P('kvh', 'req'), may hold values from -0.125 to 0.125
- w_down: bfloat16 [9728, 2560], P('req', 'kvh'), may hold values from -0.0625 to 0.0625
- kv_pool: bfloat16 [1024, 8, 128, 256], P('req', 'kvh'), may hold values from -6 to 6
- lengths: int32 [128], replicated, may hold values from 1 to 1023, as said below
- page_table: int32 [128, 8], P('req'), may hold values from 0 to 63, as said below
- new_order: int32 [128], replicated, may hold values from 0 to 127, as said below
Outputs:
- output: bfloat16 [128, 2560], P('req', 'kvh')
- new_pool: bfloat16 [1024, 8, 128, 256], P('req', 'kvh')
The draws below stay inside these ranges and needn't reach their ends.
Inputs may be any that keep to these rules, and one draw needn't show every extreme that they name: `lengths`: each request has at least one cached position and room for the new one; some request has exactly 1023. `page_table`: the 8 rows of one device name each of its 64 pool rows exactly once. `new_order`: A permutation of the requests; slot s lies on the device s // 8. The 8 requests of one device go to 8 different devices, and each device receives its 8 requests from 8 different devices.
All inputs are finite; a program needn't handle non-finite values.
Results may differ from the reference program's by a relative error of at most 0.0087.
Values may be sent and summed in bfloat16 or wider, within the bound.
No kernel may reach another device: no remote copies, remote signals or barrier semaphores. Data moves between devices by JAX's collectives and lax.ppermute only.
A program may use at most 128 MiB of HBM per device.

```python
import math
import jax
import jax.numpy as jnp
from jax import lax

D = 2560
QH = 32
KVH = 8
HD = 128
FF = 9728
R_DEV = 8
PAGE = 128
PAGES_REQ = 8
MAXLEN = 1024
REQS = 128
POOL = 1024
N_REQ = 16


def draw_lengths(key, part):
    key_caps, key_draw, key_star = jax.random.split(key, 3)
    owners = REQS // R_DEV
    device_caps = jax.random.randint(key_caps, (owners,), MAXLEN // 8, MAXLEN)
    cap_rows = jnp.repeat(device_caps, R_DEV)
    raw_draw = jax.random.randint(key_draw, (REQS,), 0, 1 << 20)
    result = 1 + raw_draw % cap_rows
    chosen = jax.random.randint(key_star, (), 0, REQS)
    return jnp.where(jnp.arange(REQS) == chosen, MAXLEN - 1, result).astype(jnp.int32)


def draw_page_table(key, part):
    owners = REQS // R_DEV
    device_keys = jax.random.split(key, owners)
    shuffled = jax.vmap(lambda single_key: jax.random.permutation(single_key, R_DEV * PAGES_REQ))(device_keys)
    return shuffled.reshape(REQS, PAGES_REQ).astype(jnp.int32)


def draw_new_order(key, part):
    owners = REQS // R_DEV
    key_sigma, key_offsets, key_slots = jax.random.split(key, 3)
    sigma = jax.random.permutation(key_sigma, owners)
    offsets = jax.random.permutation(key_offsets, owners)[:R_DEV]
    slot_keys = jax.random.split(key_slots, owners)
    slot_orders = jax.vmap(lambda single_key: jax.random.permutation(single_key, R_DEV))(slot_keys)
    sources = jnp.arange(owners, dtype=jnp.int32)[:, None]
    ranks = jnp.arange(R_DEV, dtype=jnp.int32)[None, :]
    target = sigma[(sources + offsets[None, :]) % owners]
    target_slot = slot_orders[target, ranks]
    position = (target * R_DEV + target_slot).reshape(REQS)
    return jnp.zeros((REQS,), jnp.int32).at[position].set(jnp.arange(REQS, dtype=jnp.int32))


def level_of(key, extent, pieces, low, top_value):
    gain, own = 1.0, jax.random.fold_in(key, 6)
    for axis_at, parts in pieces:
        heights = jnp.exp(jax.random.uniform(jax.random.fold_in(own, axis_at), (parts,), jnp.float32, low / len(pieces), top_value / len(pieces)))
        gain = gain * jnp.repeat(heights, extent[axis_at] // parts).reshape([-1 if axis == axis_at else 1 for axis in range(len(extent))])
    return gain


def noise(key, shape, scale, bound, pieces=(), kind=jnp.bfloat16):
    entries = jax.random.normal(key, shape, jnp.float32) * scale
    if len(pieces) > 0:
        entries = level_of(key, shape, pieces, -0.22, 0.18) * entries
    return jnp.clip(entries, min=-bound, max=bound).astype(kind)


def setup_inputs(seed: int = 0) -> dict:
    streams_of = jax.random.split(jax.random.key(seed), 17)
    states = noise(streams_of[0], (REQS, D), 1.0, 6.0, ((0, 16), (1, 8)))
    attn_gain = jnp.clip(1.0 + 0.18 * jax.random.normal(streams_of[1], (D,), jnp.float32), 0.099609375, 1.8984375).astype(jnp.bfloat16)
    w_query = noise(streams_of[2], (D, QH * HD), D ** -0.5, 0.125, ((1, 8),))
    w_key = noise(streams_of[3], (D, KVH * HD), D ** -0.5, 0.125, ((1, 8),))
    w_value = noise(streams_of[4], (D, KVH * HD), D ** -0.5, 0.125, ((1, 8),))
    query_gain = jnp.clip(jnp.exp(jax.random.uniform(streams_of[5], (HD,), jnp.float32, math.log(0.5), math.log(2.0))), 0.5, 2.0).astype(jnp.bfloat16)
    key_gain = jnp.clip(jnp.exp(jax.random.uniform(streams_of[6], (HD,), jnp.float32, math.log(0.5), math.log(2.0))), 0.5, 2.0).astype(jnp.bfloat16)
    w_output = noise(streams_of[7], (QH * HD, D), (HD * 4) ** -0.5, 0.25, ((0, 8),))
    ffn_gain = jnp.clip(1.0 + 0.18 * jax.random.normal(streams_of[8], (D,), jnp.float32), 0.099609375, 1.8984375).astype(jnp.bfloat16)
    w_gate = noise(streams_of[9], (D, FF), D ** -0.5, 0.125, ((0, 8), (1, 16)))
    w_up = noise(streams_of[10], (D, FF), D ** -0.5, 0.125, ((0, 8), (1, 16)))
    w_down = noise(streams_of[11], (FF, D), FF ** -0.5, 0.0625, ((0, 16), (1, 8)))
    kv_pool = noise(streams_of[12], (POOL, KVH, PAGE, 2 * HD), 1.0, 6.0, ((0, 16), (1, 8)))
    lengths = draw_lengths(jax.random.fold_in(streams_of[16], 71), 0)
    page_table = draw_page_table(jax.random.fold_in(streams_of[16], 71), 0)
    new_order = draw_new_order(jax.random.fold_in(streams_of[16], 71), 0)
    return dict(states=states, attn_gain=attn_gain, w_query=w_query, w_key=w_key, w_value=w_value, query_gain=query_gain, key_gain=key_gain, w_output=w_output, ffn_gain=ffn_gain, w_gate=w_gate, w_up=w_up, w_down=w_down, kv_pool=kv_pool, lengths=lengths, page_table=page_table, new_order=new_order)


EPSILON = 1e-06

def rms_norm(values, norm_gain):
    mean_sq = lax.optimization_barrier(jnp.mean(values * values, axis=-1, keepdims=True))
    return values * lax.rsqrt(mean_sq + EPSILON) * norm_gain

def rotary(values, positions):
    half_dim = values.shape[-1] // 2
    frequency = jnp.exp(jnp.arange(half_dim, dtype=jnp.float32) * (-2.0 * math.log(1000000.0) / values.shape[-1]))
    angles = positions.astype(jnp.float32)[:, None, None] * frequency
    cosine = jnp.cos(angles)
    sine_part = jnp.sin(angles)
    first_half = values[..., :half_dim]
    second_half = values[..., half_dim:]
    return jnp.concatenate([first_half * cosine - second_half * sine_part, second_half * cosine + first_half * sine_part], axis=-1)

def reference(states, attn_gain, w_query, w_key, w_value, query_gain, key_gain, w_output, ffn_gain, w_gate, w_up, w_down, kv_pool, lengths, page_table, new_order):
    group_size = QH // KVH
    channels = 2 * HD
    inputs = states.astype(jnp.float32)
    normed = rms_norm(inputs, attn_gain.astype(jnp.float32)).astype(jnp.bfloat16)
    query = jnp.dot(normed, w_query, preferred_element_type=jnp.float32).reshape(REQS, QH, HD)
    key_new = jnp.dot(normed, w_key, preferred_element_type=jnp.float32).reshape(REQS, KVH, HD)
    value_new = jnp.dot(normed, w_value, preferred_element_type=jnp.float32).reshape(REQS, KVH, HD)
    query = rotary(rms_norm(query, query_gain.astype(jnp.float32)), lengths).astype(jnp.bfloat16)
    key_new = rotary(rms_norm(key_new, key_gain.astype(jnp.float32)), lengths).astype(jnp.bfloat16)
    fresh = jnp.concatenate([key_new, value_new.astype(jnp.bfloat16)], axis=-1)
    pool_owner = kv_pool.reshape(N_REQ, R_DEV * PAGES_REQ, KVH, PAGE, channels)
    positions = jnp.arange(MAXLEN, dtype=jnp.int32)
    scale_factor = 1.0 / math.sqrt(HD)

    def one_slot(slot):
        request = new_order[slot]
        owner_pages = pool_owner[request // R_DEV]
        page_rows = owner_pages[page_table[request]]
        sequence = page_rows.transpose(1, 0, 2, 3).reshape(KVH, MAXLEN, channels)
        length_now = lengths[request]
        kept = positions[None, :, None] < length_now
        placed = positions[None, :, None] == length_now
        sequence = jnp.where(kept, sequence, jnp.where(placed, fresh[request][:, None, :], jnp.zeros_like(sequence)))
        queries_one = query[request].astype(jnp.float32).reshape(KVH, group_size, HD)
        scores = jnp.einsum('kgd,ktd->kgt', queries_one, sequence[..., :HD].astype(jnp.float32)) * scale_factor
        scores = jnp.where(positions[None, None, :] <= length_now, scores, -jnp.inf)
        weights = jax.nn.softmax(scores, axis=-1).astype(jnp.bfloat16)
        mixed = jnp.einsum('kgt,ktd->kgd', weights.astype(jnp.float32), sequence[..., HD:].astype(jnp.float32))
        block = sequence.reshape(KVH, PAGES_REQ, PAGE, channels).transpose(1, 0, 2, 3)
        return (block, mixed.reshape(QH * HD).astype(jnp.bfloat16))
    blocks, attended = lax.map(one_slot, jnp.arange(REQS, dtype=jnp.int32))
    new_pool = blocks.reshape(POOL, KVH, PAGE, channels)
    attention = jnp.zeros((REQS, QH * HD), jnp.bfloat16).at[new_order].set(attended)
    residual = (inputs + jnp.dot(attention, w_output, preferred_element_type=jnp.float32)).astype(jnp.bfloat16)
    residual_wide = residual.astype(jnp.float32)
    normed_two = rms_norm(residual_wide, ffn_gain.astype(jnp.float32)).astype(jnp.bfloat16)
    gate = jnp.dot(normed_two, w_gate, preferred_element_type=jnp.float32)
    upward = jnp.dot(normed_two, w_up, preferred_element_type=jnp.float32)
    hidden = (jax.nn.silu(gate) * upward).astype(jnp.bfloat16)
    output = (residual_wide + jnp.dot(hidden, w_down, preferred_element_type=jnp.float32)).astype(jnp.bfloat16)
    return (output, new_pool)
```

```python
import math

import jax
import jax.numpy as jnp
from jax import lax
from jax.sharding import PartitionSpec as P

D = 2560


EPSILON = 1e-06


def rms_norm(values, norm_gain):
    mean_sq = jnp.mean(values * values, axis=-1, keepdims=True)
    return values * lax.rsqrt(mean_sq + EPSILON) * norm_gain


def rotary(values, positions):
    half_dim = values.shape[-1] // 2
    frequency = jnp.exp(
        jnp.arange(half_dim, dtype=jnp.float32) * (-2.0 * math.log(1000000.0) / values.shape[-1])
    )
    angles = positions.astype(jnp.float32)[:, None, None] * frequency
    cosine = jnp.cos(angles)
    sine_part = jnp.sin(angles)
    first_half = values[..., :half_dim]
    second_half = values[..., half_dim:]
    return jnp.concatenate(
        [
            first_half * cosine - second_half * sine_part,
            second_half * cosine + first_half * sine_part,
        ],
        axis=-1,
    )


def mask_blocks(blocks, lengths_now, fresh):
    row_count, pages_per, kv_local, page_len, channels = blocks.shape
    positions = (
        jnp.arange(pages_per, dtype=jnp.int32)[:, None] * page_len
        + jnp.arange(page_len, dtype=jnp.int32)[None, :]
    )
    positions = positions[None, :, None, :, None]
    lengths_col = lengths_now[:, None, None, None, None]
    kept = positions < lengths_col
    placed = positions == lengths_col
    return jnp.where(
        kept,
        blocks,
        jnp.where(placed, fresh[:, None, :, None, :], jnp.zeros((), jnp.bfloat16)),
    )


def attend(query, sequence, lengths_now):
    row_count, kv_local, span_len, channels = sequence.shape
    head_dim = channels // 2
    q_local = query.shape[1]
    group_size = q_local // kv_local
    grouped = query.reshape(row_count, kv_local, group_size, head_dim)
    scores = jnp.einsum(
        "rkgd,rktd->rkgt", grouped, sequence[..., :head_dim], preferred_element_type=jnp.float32
    ) * (1.0 / math.sqrt(head_dim))
    positions = jnp.arange(span_len, dtype=jnp.int32)
    valid = positions[None, None, None, :] <= lengths_now[:, None, None, None]
    scores = jnp.where(valid, scores, -jnp.inf)
    weights = jax.nn.softmax(scores, axis=-1).astype(jnp.bfloat16)
    mixed = jnp.einsum(
        "rkgt,rktd->rkgd", weights, sequence[..., head_dim:], preferred_element_type=jnp.float32
    )
    return mixed.reshape(row_count, q_local * head_dim).astype(jnp.bfloat16)


def per_device(
    states,
    attn_gain,
    w_query,
    w_key,
    w_value,
    query_gain,
    key_gain,
    w_output,
    ffn_gain,
    w_gate,
    w_up,
    w_down,
    kv_pool,
    lengths,
    page_table,
    new_order,
):
    devices_req = lax.axis_size("req")
    my_index = lax.axis_index("req")
    kvh_index = lax.axis_index("kvh")
    row_count = states.shape[0]
    width_local = states.shape[1]
    head_dim = query_gain.shape[0]
    kv_local = w_key.shape[1] // head_dim
    q_local = w_query.shape[1] // head_dim
    pages_per = page_table.shape[1]
    page_len = kv_pool.shape[2]
    channels = 2 * head_dim
    total_rows = new_order.shape[0]

    everyone = jnp.arange(total_rows, dtype=jnp.int32)
    new_position = jnp.zeros((total_rows,), jnp.int32).at[new_order].set(everyone)
    home = my_index * row_count + jnp.arange(row_count, dtype=jnp.int32)
    destination = new_position[home] // row_count
    peer_ids = jnp.arange(devices_req, dtype=jnp.int32)
    matches = destination[None, :] == peer_ids[:, None]
    picked = jnp.argmax(matches.astype(jnp.int32), axis=1)
    parcels = kv_pool[page_table[picked]]
    received = lax.all_to_all(parcels, "req", split_axis=0, concat_axis=0, tiled=True)
    arriving = lax.dynamic_slice_in_dim(new_order, my_index * row_count, row_count)
    source_owner = arriving // row_count

    full_states = lax.all_gather(states, "kvh", axis=1, tiled=True)
    normed = rms_norm(full_states.astype(jnp.float32), attn_gain.astype(jnp.float32)).astype(
        jnp.bfloat16
    )
    query = jnp.dot(normed, w_query, preferred_element_type=jnp.float32).reshape(
        row_count, q_local, head_dim
    )
    key_new = jnp.dot(normed, w_key, preferred_element_type=jnp.float32).reshape(
        row_count, kv_local, head_dim
    )
    value_new = jnp.dot(normed, w_value, preferred_element_type=jnp.float32).reshape(
        row_count, kv_local, head_dim
    )
    positions_home = lengths[home]
    query = rotary(rms_norm(query, query_gain.astype(jnp.float32)), positions_home).astype(
        jnp.bfloat16
    )
    key_new = rotary(rms_norm(key_new, key_gain.astype(jnp.float32)), positions_home).astype(
        jnp.bfloat16
    )
    fresh = jnp.concatenate([key_new, value_new.astype(jnp.bfloat16)], axis=-1)
    home_blocks = mask_blocks(kv_pool[page_table], positions_home, fresh)
    sequence = home_blocks.transpose(0, 2, 1, 3, 4).reshape(
        row_count, kv_local, pages_per * page_len, channels
    )
    mixed = attend(query, sequence, positions_home)
    partial_out = jnp.dot(mixed, w_output, preferred_element_type=jnp.float32)
    attn_out = lax.psum(partial_out, "kvh")
    residual_full = (full_states.astype(jnp.float32) + attn_out).astype(jnp.bfloat16)
    residual_wide_full = residual_full.astype(jnp.float32)
    total_sq = jnp.sum(residual_wide_full * residual_wide_full, axis=-1, keepdims=True)
    residual_wide = lax.dynamic_slice_in_dim(
        residual_wide_full, kvh_index * width_local, width_local, axis=1
    )
    normed_two = (
        residual_wide * lax.rsqrt(total_sq / D + EPSILON) * ffn_gain.astype(jnp.float32)
    ).astype(jnp.bfloat16)

    fresh_flat = fresh.reshape(row_count, kv_local * channels)
    gathered = lax.all_gather(
        jnp.concatenate([normed_two, fresh_flat], axis=1), "req", axis=0, tiled=True
    )
    normed_all = gathered[:, :width_local]
    fresh_all = gathered[:, width_local:].reshape(total_rows, kv_local, channels)
    ffn_width = w_gate.shape[1]
    joined = jnp.concatenate([w_gate, w_up], axis=1)
    partial_both = jnp.dot(normed_all, joined, preferred_element_type=jnp.float32)
    summed = lax.psum(partial_both, "kvh")
    hidden = (jax.nn.silu(summed[:, :ffn_width]) * summed[:, ffn_width:]).astype(jnp.bfloat16)
    lowered = lax.psum_scatter(
        jnp.dot(hidden, w_down, preferred_element_type=jnp.float32),
        "req",
        scatter_dimension=0,
        tiled=True,
    )
    result = (residual_wide + lowered).astype(jnp.bfloat16)

    arrived = received[source_owner]
    new_blocks = mask_blocks(arrived, lengths[arriving], fresh_all[arriving])
    new_pool = new_blocks.reshape(row_count * pages_per, kv_local, page_len, channels)
    return (result, new_pool)


def solution(mesh):
    in_specs = (
        P("req", "kvh"),
        P(),
        P(None, "kvh"),
        P(None, "kvh"),
        P(None, "kvh"),
        P(),
        P(),
        P("kvh", None),
        P("kvh"),
        P("kvh", "req"),
        P("kvh", "req"),
        P("req", "kvh"),
        P("req", "kvh", None, None),
        P(),
        P("req", None),
        P(),
    )
    out_specs = (P("req", "kvh"), P("req", "kvh", None, None))
    return jax.shard_map(
        per_device, mesh=mesh, in_specs=in_specs, out_specs=out_specs, check_vma=False
    )
```

```python
import math

import jax
import jax.numpy as jnp
from jax import lax
from jax.sharding import PartitionSpec as P

D = 2560


EPSILON = 1e-06


def rms_norm(values, norm_gain):
    mean_sq = jnp.mean(values * values, axis=-1, keepdims=True)
    return values * lax.rsqrt(mean_sq + EPSILON) * norm_gain


def rotary(values, positions):
    half_dim = values.shape[-1] // 2
    frequency = jnp.exp(
        jnp.arange(half_dim, dtype=jnp.float32) * (-2.0 * math.log(1000000.0) / values.shape[-1])
    )
    angles = positions.astype(jnp.float32)[:, None, None] * frequency
    cosine = jnp.cos(angles)
    sine_part = jnp.sin(angles)
    first_half = values[..., :half_dim]
    second_half = values[..., half_dim:]
    return jnp.concatenate(
        [
            first_half * cosine - second_half * sine_part,
            second_half * cosine + first_half * sine_part,
        ],
        axis=-1,
    )


def mask_blocks(blocks, lengths_now, fresh):
    row_count, pages_per, kv_local, page_len, channels = blocks.shape
    positions = (
        jnp.arange(pages_per, dtype=jnp.int32)[:, None] * page_len
        + jnp.arange(page_len, dtype=jnp.int32)[None, :]
    )
    positions = positions[None, :, None, :, None]
    lengths_col = lengths_now[:, None, None, None, None]
    kept = positions < lengths_col
    placed = positions == lengths_col
    return jnp.where(
        kept,
        blocks,
        jnp.where(placed, fresh[:, None, :, None, :], jnp.zeros((), jnp.bfloat16)),
    )


def attend(query, sequence, lengths_now):
    row_count, kv_local, span_len, channels = sequence.shape
    head_dim = channels // 2
    q_local = query.shape[1]
    group_size = q_local // kv_local
    grouped = query.reshape(row_count, kv_local, group_size, head_dim)
    scores = jnp.einsum(
        "rkgd,rktd->rkgt", grouped, sequence[..., :head_dim], preferred_element_type=jnp.float32
    ) * (1.0 / math.sqrt(head_dim))
    positions = jnp.arange(span_len, dtype=jnp.int32)
    valid = positions[None, None, None, :] <= lengths_now[:, None, None, None]
    scores = jnp.where(valid, scores, -jnp.inf)
    weights = jax.nn.softmax(scores, axis=-1).astype(jnp.bfloat16)
    mixed = jnp.einsum(
        "rkgt,rktd->rkgd", weights, sequence[..., head_dim:], preferred_element_type=jnp.float32
    )
    return mixed.reshape(row_count, q_local * head_dim).astype(jnp.bfloat16)


def per_device(
    states,
    attn_gain,
    w_query,
    w_key,
    w_value,
    query_gain,
    key_gain,
    w_output,
    ffn_gain,
    w_gate,
    w_up,
    w_down,
    kv_pool,
    lengths,
    page_table,
    new_order,
):
    devices_req = lax.axis_size("req")
    my_index = lax.axis_index("req")
    kvh_index = lax.axis_index("kvh")
    row_count = states.shape[0]
    width_local = states.shape[1]
    head_dim = query_gain.shape[0]
    kv_local = w_key.shape[1] // head_dim
    q_local = w_query.shape[1] // head_dim
    pages_per = page_table.shape[1]
    page_len = kv_pool.shape[2]
    channels = 2 * head_dim
    total_rows = new_order.shape[0]

    everyone = jnp.arange(total_rows, dtype=jnp.int32)
    new_position = jnp.zeros((total_rows,), jnp.int32).at[new_order].set(everyone)
    home = my_index * row_count + jnp.arange(row_count, dtype=jnp.int32)
    destination = new_position[home] // row_count
    peer_ids = jnp.arange(devices_req, dtype=jnp.int32)
    matches = destination[None, :] == peer_ids[:, None]
    picked = jnp.argmax(matches.astype(jnp.int32), axis=1)
    parcels = kv_pool[page_table[picked]]
    received = lax.all_to_all(parcels, "req", split_axis=0, concat_axis=0, tiled=True)
    arriving = lax.dynamic_slice_in_dim(new_order, my_index * row_count, row_count)
    source_owner = arriving // row_count

    full_states = lax.all_gather(states, "kvh", axis=1, tiled=True)
    normed = rms_norm(full_states.astype(jnp.float32), attn_gain.astype(jnp.float32)).astype(
        jnp.bfloat16
    )
    query = jnp.dot(normed, w_query, preferred_element_type=jnp.float32).reshape(
        row_count, q_local, head_dim
    )
    key_new = jnp.dot(normed, w_key, preferred_element_type=jnp.float32).reshape(
        row_count, kv_local, head_dim
    )
    value_new = jnp.dot(normed, w_value, preferred_element_type=jnp.float32).reshape(
        row_count, kv_local, head_dim
    )
    positions_home = lengths[home]
    query = rotary(rms_norm(query, query_gain.astype(jnp.float32)), positions_home).astype(
        jnp.bfloat16
    )
    key_new = rotary(rms_norm(key_new, key_gain.astype(jnp.float32)), positions_home).astype(
        jnp.bfloat16
    )
    fresh = jnp.concatenate([key_new, value_new.astype(jnp.bfloat16)], axis=-1)
    home_blocks = mask_blocks(kv_pool[page_table], positions_home, fresh)
    sequence = home_blocks.transpose(0, 2, 1, 3, 4).reshape(
        row_count, kv_local, pages_per * page_len, channels
    )
    mixed = attend(query, sequence, positions_home)
    partial_out = jnp.dot(mixed, w_output, preferred_element_type=jnp.float32)
    devices_kvh = lax.axis_size("kvh")
    attn_out = jnp.sum(
        lax.all_to_all(
            jnp.broadcast_to(partial_out[None], (devices_kvh,) + partial_out.shape),
            "kvh",
            split_axis=0,
            concat_axis=0,
            tiled=True,
        ),
        axis=0,
    )
    residual_full = (full_states.astype(jnp.float32) + attn_out).astype(jnp.bfloat16)
    residual_wide_full = residual_full.astype(jnp.float32)
    total_sq = jnp.sum(residual_wide_full * residual_wide_full, axis=-1, keepdims=True)
    residual_wide = lax.dynamic_slice_in_dim(
        residual_wide_full, kvh_index * width_local, width_local, axis=1
    )
    normed_two = (
        residual_wide * lax.rsqrt(total_sq / D + EPSILON) * ffn_gain.astype(jnp.float32)
    ).astype(jnp.bfloat16)

    fresh_flat = fresh.reshape(row_count, kv_local * channels)
    gathered = lax.all_gather(
        jnp.concatenate([normed_two, fresh_flat], axis=1), "req", axis=0, tiled=True
    )
    normed_all = gathered[:, :width_local]
    fresh_all = gathered[:, width_local:].reshape(total_rows, kv_local, channels)
    ffn_width = w_gate.shape[1]
    joined = jnp.concatenate([w_gate, w_up], axis=1)
    partial_both = jnp.dot(normed_all, joined, preferred_element_type=jnp.float32)
    group_rows = total_rows // devices_kvh
    summed = jnp.sum(
        lax.all_to_all(
            partial_both.reshape(devices_kvh, group_rows, 2 * ffn_width),
            "kvh",
            split_axis=0,
            concat_axis=0,
            tiled=True,
        ),
        axis=0,
    )
    hidden_part = (jax.nn.silu(summed[:, :ffn_width]) * summed[:, ffn_width:]).astype(
        jnp.bfloat16
    )
    hidden = lax.all_gather(hidden_part, "kvh", axis=0, tiled=True)
    lowered_parts = jnp.dot(hidden, w_down, preferred_element_type=jnp.float32)
    lowered = jnp.sum(
        lax.all_to_all(
            lowered_parts.reshape(devices_req, row_count, width_local),
            "req",
            split_axis=0,
            concat_axis=0,
            tiled=True,
        ),
        axis=0,
    )
    result = (residual_wide + lowered).astype(jnp.bfloat16)

    arrived = received[source_owner]
    new_blocks = mask_blocks(arrived, lengths[arriving], fresh_all[arriving])
    new_pool = new_blocks.reshape(row_count * pages_per, kv_local, page_len, channels)
    return (result, new_pool)


def solution(mesh):
    in_specs = (
        P("req", "kvh"),
        P(),
        P(None, "kvh"),
        P(None, "kvh"),
        P(None, "kvh"),
        P(),
        P(),
        P("kvh", None),
        P("kvh"),
        P("kvh", "req"),
        P("kvh", "req"),
        P("req", "kvh"),
        P("req", "kvh", None, None),
        P(),
        P("req", None),
        P(),
    )
    out_specs = (P("req", "kvh"), P("req", "kvh", None, None))
    return jax.shard_map(
        per_device, mesh=mesh, in_specs=in_specs, out_specs=out_specs, check_vma=False
    )
```

```python
import math

import jax
import jax.numpy as jnp
from jax import lax
from jax.sharding import PartitionSpec as P


D = 2560


EPSILON = 1e-06


def rms_norm(values, norm_gain):
    mean_sq = jnp.mean(values * values, axis=-1, keepdims=True)
    return values * lax.rsqrt(mean_sq + EPSILON) * norm_gain


def rotary(values, positions):
    half_dim = values.shape[-1] // 2
    frequency = jnp.exp(
        jnp.arange(half_dim, dtype=jnp.float32) * (-2.0 * math.log(1000000.0) / values.shape[-1])
    )
    angles = positions.astype(jnp.float32)[:, None, None] * frequency
    cosine = jnp.cos(angles)
    sine_part = jnp.sin(angles)
    first_half = values[..., :half_dim]
    second_half = values[..., half_dim:]
    return jnp.concatenate(
        [
            first_half * cosine - second_half * sine_part,
            second_half * cosine + first_half * sine_part,
        ],
        axis=-1,
    )


def mask_blocks(blocks, lengths_now, fresh):
    _, pages_per, _, page_len, _ = blocks.shape
    positions = (
        jnp.arange(pages_per, dtype=jnp.int32)[:, None] * page_len
        + jnp.arange(page_len, dtype=jnp.int32)[None, :]
    )
    positions = positions[None, :, None, :, None]
    lengths_col = lengths_now[:, None, None, None, None]
    kept = positions < lengths_col
    placed = positions == lengths_col
    return jnp.where(
        kept,
        blocks,
        jnp.where(placed, fresh[:, None, :, None, :], jnp.zeros((), jnp.bfloat16)),
    )


def attend(query, sequence, lengths_now):
    row_count, kv_local, span_len, channels = sequence.shape
    head_dim = channels // 2
    q_local = query.shape[1]
    group_size = q_local // kv_local
    grouped = query.reshape(row_count, kv_local, group_size, head_dim)
    scores = jnp.einsum(
        "rkgd,rktd->rkgt", grouped, sequence[..., :head_dim], preferred_element_type=jnp.float32
    ) * (1.0 / math.sqrt(head_dim))
    positions = jnp.arange(span_len, dtype=jnp.int32)
    valid = positions[None, None, None, :] <= lengths_now[:, None, None, None]
    scores = jnp.where(valid, scores, -jnp.inf)
    weights = jax.nn.softmax(scores, axis=-1).astype(jnp.bfloat16)
    mixed = jnp.einsum(
        "rkgt,rktd->rkgd", weights, sequence[..., head_dim:], preferred_element_type=jnp.float32
    )
    return mixed.reshape(row_count, q_local * head_dim).astype(jnp.bfloat16)


def per_device(
    states,
    attn_gain,
    w_query,
    w_key,
    w_value,
    query_gain,
    key_gain,
    w_output,
    ffn_gain,
    w_gate,
    w_up,
    w_down,
    kv_pool,
    lengths,
    page_table,
    new_order,
):
    devices_req = lax.axis_size("req")
    my_index = lax.axis_index("req")
    kvh_index = lax.axis_index("kvh")
    row_count = states.shape[0]
    width_local = states.shape[1]
    head_dim = query_gain.shape[0]
    kv_local = w_key.shape[1] // head_dim
    q_local = w_query.shape[1] // head_dim
    pages_per = page_table.shape[1]
    page_len = kv_pool.shape[2]
    channels = 2 * head_dim
    total_rows = new_order.shape[0]

    everyone = jnp.arange(total_rows, dtype=jnp.int32)
    new_position = jnp.zeros((total_rows,), jnp.int32).at[new_order].set(everyone)
    home = my_index * row_count + jnp.arange(row_count, dtype=jnp.int32)
    destination = new_position[home] // row_count
    peer_ids = jnp.arange(devices_req, dtype=jnp.int32)
    matches = destination[None, :] == peer_ids[:, None]
    picked = jnp.argmax(matches.astype(jnp.int32), axis=1)
    shift_parcels = [
        kv_pool[page_table[picked[(my_index + shift) % devices_req]]]
        for shift in range(devices_req)
    ]
    early_shifts = devices_req // 3
    arriving = lax.dynamic_slice_in_dim(new_order, my_index * row_count, row_count)
    source_owner = arriving // row_count

    full_states = lax.all_gather(states, "kvh", axis=1, tiled=True)
    normed = rms_norm(full_states.astype(jnp.float32), attn_gain.astype(jnp.float32)).astype(
        jnp.bfloat16
    )
    query = jnp.dot(normed, w_query, preferred_element_type=jnp.float32).reshape(
        row_count, q_local, head_dim
    )
    key_new = jnp.dot(normed, w_key, preferred_element_type=jnp.float32).reshape(
        row_count, kv_local, head_dim
    )
    value_new = jnp.dot(normed, w_value, preferred_element_type=jnp.float32).reshape(
        row_count, kv_local, head_dim
    )
    positions_home = lengths[home]
    query = rotary(rms_norm(query, query_gain.astype(jnp.float32)), positions_home).astype(
        jnp.bfloat16
    )
    key_new = rotary(rms_norm(key_new, key_gain.astype(jnp.float32)), positions_home).astype(
        jnp.bfloat16
    )
    fresh = jnp.concatenate([key_new, value_new.astype(jnp.bfloat16)], axis=-1)
    home_blocks = mask_blocks(kv_pool[page_table], positions_home, fresh)
    sequence = home_blocks.transpose(0, 2, 1, 3, 4).reshape(
        row_count, kv_local, pages_per * page_len, channels
    )
    mixed = attend(query, sequence, positions_home)
    partial_out = jnp.dot(mixed, w_output, preferred_element_type=jnp.float32)
    devices_kvh = lax.axis_size("kvh")
    attn_out = jnp.sum(
        lax.all_to_all(
            jnp.broadcast_to(partial_out[None], (devices_kvh,) + partial_out.shape),
            "kvh",
            split_axis=0,
            concat_axis=0,
            tiled=True,
        ),
        axis=0,
    )
    residual_full = (full_states.astype(jnp.float32) + attn_out).astype(jnp.bfloat16)
    residual_wide_full = residual_full.astype(jnp.float32)
    total_sq = jnp.sum(residual_wide_full * residual_wide_full, axis=-1, keepdims=True)
    residual_wide = lax.dynamic_slice_in_dim(
        residual_wide_full, kvh_index * width_local, width_local, axis=1
    )
    normed_two = (
        residual_wide * lax.rsqrt(total_sq / D + EPSILON) * ffn_gain.astype(jnp.float32)
    ).astype(jnp.bfloat16)

    fresh_flat = fresh.reshape(row_count, kv_local * channels)
    gathered = lax.all_gather(
        jnp.concatenate([normed_two, fresh_flat], axis=1), "req", axis=0, tiled=True
    )
    late_parcels = shift_parcels[early_shifts + 1 :]
    gathered, late_parcels = lax.optimization_barrier((gathered, late_parcels))
    shift_parcels = shift_parcels[: early_shifts + 1] + list(late_parcels)
    normed_all = gathered[:, :width_local]
    fresh_all = gathered[:, width_local:].reshape(total_rows, kv_local, channels)
    ffn_width = w_gate.shape[1]
    joined = jnp.concatenate([w_gate, w_up], axis=1)
    partial_both = jnp.dot(normed_all, joined, preferred_element_type=jnp.float32)
    group_rows = total_rows // devices_kvh
    summed = jnp.sum(
        lax.all_to_all(
            partial_both.reshape(devices_kvh, group_rows, 2 * ffn_width),
            "kvh",
            split_axis=0,
            concat_axis=0,
            tiled=True,
        ),
        axis=0,
    )
    hidden_part = (jax.nn.silu(summed[:, :ffn_width]) * summed[:, ffn_width:]).astype(
        jnp.bfloat16
    )
    hidden = lax.all_gather(hidden_part, "kvh", axis=0, tiled=True)
    lowered_parts = jnp.dot(hidden, w_down, preferred_element_type=jnp.float32)
    lowered_all = lax.all_to_all(
        lowered_parts.reshape(devices_req, row_count, width_local),
        "req",
        split_axis=0,
        concat_axis=0,
        tiled=True,
    )
    result = (residual_wide + jnp.sum(lowered_all, axis=0)).astype(jnp.bfloat16)

    moved = [shift_parcels[0]]
    for shift in range(1, devices_req):
        moved.append(
            lax.ppermute(
                shift_parcels[shift],
                "req",
                [(i, (i + shift) % devices_req) for i in range(devices_req)],
            )
        )
    received = jnp.stack(moved)
    arrived = received[(my_index - source_owner) % devices_req]
    new_blocks = mask_blocks(arrived, lengths[arriving], fresh_all[arriving])
    new_pool = new_blocks.reshape(row_count * pages_per, kv_local, page_len, channels)
    return (result, new_pool)


def solution(mesh):
    in_specs = (
        P("req", "kvh"),
        P(),
        P(None, "kvh"),
        P(None, "kvh"),
        P(None, "kvh"),
        P(),
        P(),
        P("kvh", None),
        P("kvh"),
        P("kvh", "req"),
        P("kvh", "req"),
        P("req", "kvh"),
        P("req", "kvh", None, None),
        P(),
        P("req", None),
        P(),
    )
    out_specs = (P("req", "kvh"), P("req", "kvh", None, None))

    return jax.shard_map(
        per_device, mesh=mesh, in_specs=in_specs, out_specs=out_specs, check_vma=False
    )
```

```python
import math

import jax
import jax.numpy as jnp
from jax import lax
from jax.sharding import PartitionSpec as P

D = 2560


EPSILON = 1e-06


def rms_norm(values, norm_gain):
    mean_sq = jnp.mean(values * values, axis=-1, keepdims=True)
    return values * lax.rsqrt(mean_sq + EPSILON) * norm_gain


def rotary(values, positions):
    half_dim = values.shape[-1] // 2
    frequency = jnp.exp(
        jnp.arange(half_dim, dtype=jnp.float32) * (-2.0 * math.log(1000000.0) / values.shape[-1])
    )
    angles = positions.astype(jnp.float32)[:, None, None] * frequency
    cosine = jnp.cos(angles)
    sine_part = jnp.sin(angles)
    first_half = values[..., :half_dim]
    second_half = values[..., half_dim:]
    return jnp.concatenate(
        [
            first_half * cosine - second_half * sine_part,
            second_half * cosine + first_half * sine_part,
        ],
        axis=-1,
    )


def mask_blocks(blocks, lengths_now, fresh):
    row_count, pages_per, kv_local, page_len, channels = blocks.shape
    positions = (
        jnp.arange(pages_per, dtype=jnp.int32)[:, None] * page_len
        + jnp.arange(page_len, dtype=jnp.int32)[None, :]
    )
    positions = positions[None, :, None, :, None]
    lengths_col = lengths_now[:, None, None, None, None]
    kept = positions < lengths_col
    placed = positions == lengths_col
    return jnp.where(
        kept,
        blocks,
        jnp.where(placed, fresh[:, None, :, None, :], jnp.zeros((), jnp.bfloat16)),
    )


def attend(query, sequence, lengths_now):
    row_count, kv_local, span_len, channels = sequence.shape
    head_dim = channels // 2
    q_local = query.shape[1]
    group_size = q_local // kv_local
    grouped = query.reshape(row_count, kv_local, group_size, head_dim)
    scores = jnp.einsum(
        "rkgd,rktd->rkgt", grouped, sequence[..., :head_dim], preferred_element_type=jnp.float32
    ) * (1.0 / math.sqrt(head_dim))
    positions = jnp.arange(span_len, dtype=jnp.int32)
    valid = positions[None, None, None, :] <= lengths_now[:, None, None, None]
    scores = jnp.where(valid, scores, -jnp.inf)
    weights = jax.nn.softmax(scores, axis=-1).astype(jnp.bfloat16)
    mixed = jnp.einsum(
        "rkgt,rktd->rkgd", weights, sequence[..., head_dim:], preferred_element_type=jnp.float32
    )
    return mixed.reshape(row_count, q_local * head_dim).astype(jnp.bfloat16)


def per_device(
    states,
    attn_gain,
    w_query,
    w_key,
    w_value,
    query_gain,
    key_gain,
    w_output,
    ffn_gain,
    w_gate,
    w_up,
    w_down,
    kv_pool,
    lengths,
    page_table,
    new_order,
):
    devices_req = lax.axis_size("req")
    my_index = lax.axis_index("req")
    kvh_index = lax.axis_index("kvh")
    row_count = states.shape[0]
    width_local = states.shape[1]
    head_dim = query_gain.shape[0]
    kv_local = w_key.shape[1] // head_dim
    q_local = w_query.shape[1] // head_dim
    pages_per = page_table.shape[1]
    page_len = kv_pool.shape[2]
    channels = 2 * head_dim
    total_rows = new_order.shape[0]

    everyone = jnp.arange(total_rows, dtype=jnp.int32)
    new_position = jnp.zeros((total_rows,), jnp.int32).at[new_order].set(everyone)
    home = my_index * row_count + jnp.arange(row_count, dtype=jnp.int32)
    destination = new_position[home] // row_count
    peer_ids = jnp.arange(devices_req, dtype=jnp.int32)
    matches = destination[None, :] == peer_ids[:, None]
    picked = jnp.argmax(matches.astype(jnp.int32), axis=1)
    parcels = kv_pool[page_table[picked]]
    received = lax.all_to_all(parcels, "req", split_axis=0, concat_axis=0, tiled=True)
    arriving = lax.dynamic_slice_in_dim(new_order, my_index * row_count, row_count)
    source_owner = arriving // row_count

    full_states = lax.all_gather(states, "kvh", axis=1, tiled=True)
    normed = rms_norm(full_states.astype(jnp.float32), attn_gain.astype(jnp.float32)).astype(
        jnp.bfloat16
    )
    query = jnp.dot(normed, w_query, preferred_element_type=jnp.float32).reshape(
        row_count, q_local, head_dim
    )
    key_new = jnp.dot(normed, w_key, preferred_element_type=jnp.float32).reshape(
        row_count, kv_local, head_dim
    )
    value_new = jnp.dot(normed, w_value, preferred_element_type=jnp.float32).reshape(
        row_count, kv_local, head_dim
    )
    positions_home = lengths[home]
    query = rotary(rms_norm(query, query_gain.astype(jnp.float32)), positions_home).astype(
        jnp.bfloat16
    )
    key_new = rotary(rms_norm(key_new, key_gain.astype(jnp.float32)), positions_home).astype(
        jnp.bfloat16
    )
    fresh = jnp.concatenate([key_new, value_new.astype(jnp.bfloat16)], axis=-1)
    home_blocks = mask_blocks(kv_pool[page_table], positions_home, fresh)
    sequence = home_blocks.transpose(0, 2, 1, 3, 4).reshape(
        row_count, kv_local, pages_per * page_len, channels
    )
    mixed = attend(query, sequence, positions_home)
    partial_out = jnp.dot(mixed, w_output, preferred_element_type=jnp.float32)
    devices_kvh = lax.axis_size("kvh")
    attn_out = partial_out
    step = 1
    while step < devices_kvh:
        attn_out = attn_out + lax.ppermute(
            attn_out, "kvh", [(i, i ^ step) for i in range(devices_kvh)]
        )
        step *= 2
    residual_full = (full_states.astype(jnp.float32) + attn_out).astype(jnp.bfloat16)
    residual_wide_full = residual_full.astype(jnp.float32)
    total_sq = jnp.sum(residual_wide_full * residual_wide_full, axis=-1, keepdims=True)
    residual_wide = lax.dynamic_slice_in_dim(
        residual_wide_full, kvh_index * width_local, width_local, axis=1
    )
    normed_two = (
        residual_wide * lax.rsqrt(total_sq / D + EPSILON) * ffn_gain.astype(jnp.float32)
    ).astype(jnp.bfloat16)

    fresh_flat = fresh.reshape(row_count, kv_local * channels)
    outgoing = jnp.concatenate([normed_two, fresh_flat], axis=1)
    received, outgoing = lax.optimization_barrier((received, outgoing))
    gathered = lax.all_gather(outgoing, "req", axis=0, tiled=True)
    normed_all = gathered[:, :width_local]
    fresh_all = gathered[:, width_local:].reshape(total_rows, kv_local, channels)
    ffn_width = w_gate.shape[1]
    joined = jnp.concatenate([w_gate, w_up], axis=1)
    partial_both = jnp.dot(normed_all, joined, preferred_element_type=jnp.float32)
    group_rows = total_rows // devices_kvh
    summed = jnp.sum(
        lax.all_to_all(
            partial_both.reshape(devices_kvh, group_rows, 2 * ffn_width),
            "kvh",
            split_axis=0,
            concat_axis=0,
            tiled=True,
        ),
        axis=0,
    )
    hidden_part = (jax.nn.silu(summed[:, :ffn_width]) * summed[:, ffn_width:]).astype(
        jnp.bfloat16
    )
    hidden = lax.all_gather(hidden_part, "kvh", axis=0, tiled=True)
    lowered_parts = jnp.dot(hidden, w_down, preferred_element_type=jnp.float32)
    lowered = jnp.sum(
        lax.all_to_all(
            lowered_parts.reshape(devices_req, row_count, width_local),
            "req",
            split_axis=0,
            concat_axis=0,
            tiled=True,
        ),
        axis=0,
    )
    result = (residual_wide + lowered).astype(jnp.bfloat16)

    arrived = received[source_owner]
    new_blocks = mask_blocks(arrived, lengths[arriving], fresh_all[arriving])
    new_pool = new_blocks.reshape(row_count * pages_per, kv_local, page_len, channels)
    return (result, new_pool)


def solution(mesh):
    in_specs = (
        P("req", "kvh"),
        P(),
        P(None, "kvh"),
        P(None, "kvh"),
        P(None, "kvh"),
        P(),
        P(),
        P("kvh", None),
        P("kvh"),
        P("kvh", "req"),
        P("kvh", "req"),
        P("req", "kvh"),
        P("req", "kvh", None, None),
        P(),
        P("req", None),
        P(),
    )
    out_specs = (P("req", "kvh"), P("req", "kvh", None, None))
    return jax.shard_map(
        per_device, mesh=mesh, in_specs=in_specs, out_specs=out_specs, check_vma=False
    )
```

```python
import math

import jax
import jax.numpy as jnp
from jax import lax
from jax.sharding import PartitionSpec as P

D = 2560


EPSILON = 1e-06


def rms_norm(values, norm_gain):
    mean_sq = jnp.mean(values * values, axis=-1, keepdims=True)
    return values * lax.rsqrt(mean_sq + EPSILON) * norm_gain


def rotary(values, positions):
    half_dim = values.shape[-1] // 2
    frequency = jnp.exp(
        jnp.arange(half_dim, dtype=jnp.float32) * (-2.0 * math.log(1000000.0) / values.shape[-1])
    )
    angles = positions.astype(jnp.float32)[:, None, None] * frequency
    cosine = jnp.cos(angles)
    sine_part = jnp.sin(angles)
    first_half = values[..., :half_dim]
    second_half = values[..., half_dim:]
    return jnp.concatenate(
        [
            first_half * cosine - second_half * sine_part,
            second_half * cosine + first_half * sine_part,
        ],
        axis=-1,
    )


def mask_blocks(blocks, lengths_now, fresh):
    row_count, pages_per, kv_local, page_len, channels = blocks.shape
    positions = (
        jnp.arange(pages_per, dtype=jnp.int32)[:, None] * page_len
        + jnp.arange(page_len, dtype=jnp.int32)[None, :]
    )
    positions = positions[None, :, None, :, None]
    lengths_col = lengths_now[:, None, None, None, None]
    kept = positions < lengths_col
    placed = positions == lengths_col
    return jnp.where(
        kept,
        blocks,
        jnp.where(placed, fresh[:, None, :, None, :], jnp.zeros((), jnp.bfloat16)),
    )


def attend(query, sequence, lengths_now):
    row_count, kv_local, span_len, channels = sequence.shape
    head_dim = channels // 2
    q_local = query.shape[1]
    group_size = q_local // kv_local
    grouped = query.reshape(row_count, kv_local, group_size, head_dim)
    scores = jnp.einsum(
        "rkgd,rktd->rkgt", grouped, sequence[..., :head_dim], preferred_element_type=jnp.float32
    ) * (1.0 / math.sqrt(head_dim))
    positions = jnp.arange(span_len, dtype=jnp.int32)
    valid = positions[None, None, None, :] <= lengths_now[:, None, None, None]
    scores = jnp.where(valid, scores, -jnp.inf)
    weights = jax.nn.softmax(scores, axis=-1).astype(jnp.bfloat16)
    mixed = jnp.einsum(
        "rkgt,rktd->rkgd", weights, sequence[..., head_dim:], preferred_element_type=jnp.float32
    )
    return mixed.reshape(row_count, q_local * head_dim).astype(jnp.bfloat16)


def per_device(
    states,
    attn_gain,
    w_query,
    w_key,
    w_value,
    query_gain,
    key_gain,
    w_output,
    ffn_gain,
    w_gate,
    w_up,
    w_down,
    kv_pool,
    lengths,
    page_table,
    new_order,
):
    devices_req = lax.axis_size("req")
    my_index = lax.axis_index("req")
    kvh_index = lax.axis_index("kvh")
    row_count = states.shape[0]
    width_local = states.shape[1]
    head_dim = query_gain.shape[0]
    kv_local = w_key.shape[1] // head_dim
    q_local = w_query.shape[1] // head_dim
    pages_per = page_table.shape[1]
    page_len = kv_pool.shape[2]
    channels = 2 * head_dim
    total_rows = new_order.shape[0]

    everyone = jnp.arange(total_rows, dtype=jnp.int32)
    new_position = jnp.zeros((total_rows,), jnp.int32).at[new_order].set(everyone)
    home = my_index * row_count + jnp.arange(row_count, dtype=jnp.int32)
    destination = new_position[home] // row_count
    peer_ids = jnp.arange(devices_req, dtype=jnp.int32)
    matches = destination[None, :] == peer_ids[:, None]
    picked = jnp.argmax(matches.astype(jnp.int32), axis=1)
    parcels = kv_pool[page_table[picked]]
    received = lax.all_to_all(parcels, "req", split_axis=0, concat_axis=0, tiled=True)
    arriving = lax.dynamic_slice_in_dim(new_order, my_index * row_count, row_count)
    source_owner = arriving // row_count

    full_states = lax.all_gather(states, "kvh", axis=1, tiled=True)
    normed = rms_norm(full_states.astype(jnp.float32), attn_gain.astype(jnp.float32)).astype(
        jnp.bfloat16
    )
    query = jnp.dot(normed, w_query, preferred_element_type=jnp.float32).reshape(
        row_count, q_local, head_dim
    )
    key_new = jnp.dot(normed, w_key, preferred_element_type=jnp.float32).reshape(
        row_count, kv_local, head_dim
    )
    value_new = jnp.dot(normed, w_value, preferred_element_type=jnp.float32).reshape(
        row_count, kv_local, head_dim
    )
    positions_home = lengths[home]
    query = rotary(rms_norm(query, query_gain.astype(jnp.float32)), positions_home).astype(
        jnp.bfloat16
    )
    key_new = rotary(rms_norm(key_new, key_gain.astype(jnp.float32)), positions_home).astype(
        jnp.bfloat16
    )
    fresh = jnp.concatenate([key_new, value_new.astype(jnp.bfloat16)], axis=-1)
    home_blocks = mask_blocks(kv_pool[page_table], positions_home, fresh)
    sequence = home_blocks.transpose(0, 2, 1, 3, 4).reshape(
        row_count, kv_local, pages_per * page_len, channels
    )
    mixed = attend(query, sequence, positions_home)
    partial_out = jnp.dot(mixed, w_output, preferred_element_type=jnp.float32)
    devices_kvh = lax.axis_size("kvh")
    attn_out = partial_out
    step = 1
    while step < devices_kvh:
        attn_out = attn_out + lax.ppermute(
            attn_out, "kvh", [(i, i ^ step) for i in range(devices_kvh)]
        )
        step *= 2
    residual_full = (full_states.astype(jnp.float32) + attn_out).astype(jnp.bfloat16)
    residual_wide_full = residual_full.astype(jnp.float32)
    total_sq = jnp.sum(residual_wide_full * residual_wide_full, axis=-1, keepdims=True)
    residual_wide = lax.dynamic_slice_in_dim(
        residual_wide_full, kvh_index * width_local, width_local, axis=1
    )
    normed_two = (
        residual_wide * lax.rsqrt(total_sq / D + EPSILON) * ffn_gain.astype(jnp.float32)
    ).astype(jnp.bfloat16)

    fresh_flat = fresh.reshape(row_count, kv_local * channels)
    outgoing = jnp.concatenate([normed_two, fresh_flat], axis=1)
    received, outgoing = lax.optimization_barrier((received, outgoing))
    gathered = lax.all_to_all(
        jnp.broadcast_to(outgoing[None], (devices_req,) + outgoing.shape),
        "req",
        split_axis=0,
        concat_axis=0,
        tiled=True,
    ).reshape(total_rows, outgoing.shape[1])
    normed_all = gathered[:, :width_local]
    fresh_all = gathered[:, width_local:].reshape(total_rows, kv_local, channels)
    ffn_width = w_gate.shape[1]
    joined = jnp.concatenate([w_gate, w_up], axis=1)
    partial_both = jnp.dot(normed_all, joined, preferred_element_type=jnp.float32)
    group_rows = total_rows // devices_kvh
    summed = jnp.sum(
        lax.all_to_all(
            partial_both.reshape(devices_kvh, group_rows, 2 * ffn_width),
            "kvh",
            split_axis=0,
            concat_axis=0,
            tiled=True,
        ),
        axis=0,
    )
    hidden_part = (jax.nn.silu(summed[:, :ffn_width]) * summed[:, ffn_width:]).astype(
        jnp.bfloat16
    )
    hidden = lax.all_to_all(
        jnp.broadcast_to(hidden_part[None], (devices_kvh,) + hidden_part.shape),
        "kvh",
        split_axis=0,
        concat_axis=0,
        tiled=True,
    ).reshape(total_rows, ffn_width)
    lowered_parts = jnp.dot(hidden, w_down, preferred_element_type=jnp.float32)
    lowered = jnp.sum(
        lax.all_to_all(
            lowered_parts.reshape(devices_req, row_count, width_local),
            "req",
            split_axis=0,
            concat_axis=0,
            tiled=True,
        ),
        axis=0,
    )
    result = (residual_wide + lowered).astype(jnp.bfloat16)

    arrived = received[source_owner]
    new_blocks = mask_blocks(arrived, lengths[arriving], fresh_all[arriving])
    new_pool = new_blocks.reshape(row_count * pages_per, kv_local, page_len, channels)
    return (result, new_pool)


def solution(mesh):
    in_specs = (
        P("req", "kvh"),
        P(),
        P(None, "kvh"),
        P(None, "kvh"),
        P(None, "kvh"),
        P(),
        P(),
        P("kvh", None),
        P("kvh"),
        P("kvh", "req"),
        P("kvh", "req"),
        P("req", "kvh"),
        P("req", "kvh", None, None),
        P(),
        P("req", None),
        P(),
    )
    out_specs = (P("req", "kvh"), P("req", "kvh", None, None))
    return jax.shard_map(
        per_device, mesh=mesh, in_specs=in_specs, out_specs=out_specs, check_vma=False
    )
```

```python
import math

import jax
import jax.numpy as jnp
from jax import lax
from jax.experimental import pallas as pl
from jax.experimental.pallas import tpu as pltpu
from jax.sharding import PartitionSpec as P

D = 2560


EPSILON = 1e-06


def rms_norm(values, norm_gain):
    mean_sq = jnp.mean(values * values, axis=-1, keepdims=True)
    return values * lax.rsqrt(mean_sq + EPSILON) * norm_gain


def rotary(values, positions):
    half_dim = values.shape[-1] // 2
    frequency = jnp.exp(
        jnp.arange(half_dim, dtype=jnp.float32) * (-2.0 * math.log(1000000.0) / values.shape[-1])
    )
    angles = positions.astype(jnp.float32)[:, None, None] * frequency
    cosine = jnp.cos(angles)
    sine_part = jnp.sin(angles)
    first_half = values[..., :half_dim]
    second_half = values[..., half_dim:]
    return jnp.concatenate(
        [
            first_half * cosine - second_half * sine_part,
            second_half * cosine + first_half * sine_part,
        ],
        axis=-1,
    )


def mask_blocks(blocks, lengths_now, fresh):
    row_count, pages_per, kv_local, page_len, channels = blocks.shape
    positions = (
        jnp.arange(pages_per, dtype=jnp.int32)[:, None] * page_len
        + jnp.arange(page_len, dtype=jnp.int32)[None, :]
    )
    positions = positions[None, :, None, :, None]
    lengths_col = lengths_now[:, None, None, None, None]
    kept = positions < lengths_col
    placed = positions == lengths_col
    return jnp.where(
        kept,
        blocks,
        jnp.where(placed, fresh[:, None, :, None, :], jnp.zeros((), jnp.bfloat16)),
    )


def pack_parcels(kv_pool, page_table, destination, slots):
    rows, kv_local, page_len, channels = kv_pool.shape
    reqs, pages_per = page_table.shape

    def kernel(table_ref, dest_ref, pool_ref, out_ref, sems):
        copies = []
        for j in range(reqs):
            for p in range(pages_per):
                copy = pltpu.make_async_copy(
                    pool_ref.at[table_ref[j, p]],
                    out_ref.at[dest_ref[j], p],
                    sems.at[j * pages_per + p],
                )
                copy.start()
                copies.append(copy)
        for copy in copies:
            copy.wait()

    return pl.pallas_call(
        kernel,
        out_shape=jax.ShapeDtypeStruct(
            (slots, pages_per, kv_local, page_len, channels), kv_pool.dtype
        ),
        in_specs=[
            pl.BlockSpec(memory_space=pltpu.SMEM),
            pl.BlockSpec(memory_space=pltpu.SMEM),
            pl.BlockSpec(memory_space=pl.ANY),
        ],
        out_specs=pl.BlockSpec(memory_space=pl.ANY),
        scratch_shapes=[pltpu.SemaphoreType.DMA((reqs * pages_per,))],
    )(page_table, destination, kv_pool)


def attend(query, sequence, lengths_now):
    row_count, kv_local, span_len, channels = sequence.shape
    head_dim = channels // 2
    q_local = query.shape[1]
    group_size = q_local // kv_local
    grouped = query.reshape(row_count, kv_local, group_size, head_dim)
    scores = jnp.einsum(
        "rkgd,rktd->rkgt", grouped, sequence[..., :head_dim], preferred_element_type=jnp.float32
    ) * (1.0 / math.sqrt(head_dim))
    positions = jnp.arange(span_len, dtype=jnp.int32)
    valid = positions[None, None, None, :] <= lengths_now[:, None, None, None]
    scores = jnp.where(valid, scores, -jnp.inf)
    weights = jax.nn.softmax(scores, axis=-1).astype(jnp.bfloat16)
    mixed = jnp.einsum(
        "rkgt,rktd->rkgd", weights, sequence[..., head_dim:], preferred_element_type=jnp.float32
    )
    return mixed.reshape(row_count, q_local * head_dim).astype(jnp.bfloat16)


def per_device(
    states,
    attn_gain,
    w_query,
    w_key,
    w_value,
    query_gain,
    key_gain,
    w_output,
    ffn_gain,
    w_gate,
    w_up,
    w_down,
    kv_pool,
    lengths,
    page_table,
    new_order,
):
    devices_req = lax.axis_size("req")
    my_index = lax.axis_index("req")
    kvh_index = lax.axis_index("kvh")
    row_count = states.shape[0]
    width_local = states.shape[1]
    head_dim = query_gain.shape[0]
    kv_local = w_key.shape[1] // head_dim
    q_local = w_query.shape[1] // head_dim
    pages_per = page_table.shape[1]
    page_len = kv_pool.shape[2]
    channels = 2 * head_dim
    total_rows = new_order.shape[0]

    home = my_index * row_count + jnp.arange(row_count, dtype=jnp.int32)
    new_slot = jnp.argmax((new_order[None, :] == home[:, None]).astype(jnp.int32), axis=1)
    destination = (new_slot // row_count).astype(jnp.int32)
    parcels = pack_parcels(kv_pool, page_table, destination, devices_req)
    received = lax.all_to_all(parcels, "req", split_axis=0, concat_axis=0, tiled=True)
    arriving = lax.dynamic_slice_in_dim(new_order, my_index * row_count, row_count)
    source_owner = arriving // row_count

    full_states = lax.all_gather(states, "kvh", axis=1, tiled=True)
    normed = rms_norm(full_states.astype(jnp.float32), attn_gain.astype(jnp.float32)).astype(
        jnp.bfloat16
    )
    query = jnp.dot(normed, w_query, preferred_element_type=jnp.float32).reshape(
        row_count, q_local, head_dim
    )
    key_new = jnp.dot(normed, w_key, preferred_element_type=jnp.float32).reshape(
        row_count, kv_local, head_dim
    )
    value_new = jnp.dot(normed, w_value, preferred_element_type=jnp.float32).reshape(
        row_count, kv_local, head_dim
    )
    positions_home = lengths[home]
    query = rotary(rms_norm(query, query_gain.astype(jnp.float32)), positions_home).astype(
        jnp.bfloat16
    )
    key_new = rotary(rms_norm(key_new, key_gain.astype(jnp.float32)), positions_home).astype(
        jnp.bfloat16
    )
    fresh = jnp.concatenate([key_new, value_new.astype(jnp.bfloat16)], axis=-1)
    home_blocks = mask_blocks(kv_pool[page_table], positions_home, fresh)
    sequence = home_blocks.transpose(0, 2, 1, 3, 4).reshape(
        row_count, kv_local, pages_per * page_len, channels
    )
    mixed = attend(query, sequence, positions_home)
    partial_out = jnp.dot(mixed, w_output, preferred_element_type=jnp.float32)
    devices_kvh = lax.axis_size("kvh")
    attn_out = partial_out
    step = 1
    while step < devices_kvh:
        attn_out = attn_out + lax.ppermute(
            attn_out, "kvh", [(i, i ^ step) for i in range(devices_kvh)]
        )
        step *= 2
    residual_full = (full_states.astype(jnp.float32) + attn_out).astype(jnp.bfloat16)
    residual_wide_full = residual_full.astype(jnp.float32)
    total_sq = jnp.sum(residual_wide_full * residual_wide_full, axis=-1, keepdims=True)
    residual_wide = lax.dynamic_slice_in_dim(
        residual_wide_full, kvh_index * width_local, width_local, axis=1
    )
    normed_two = (
        residual_wide * lax.rsqrt(total_sq / D + EPSILON) * ffn_gain.astype(jnp.float32)
    ).astype(jnp.bfloat16)

    fresh_flat = fresh.reshape(row_count, kv_local * channels)
    outgoing = jnp.concatenate([normed_two, fresh_flat], axis=1)
    received, outgoing = lax.optimization_barrier((received, outgoing))
    gathered = lax.all_to_all(
        jnp.broadcast_to(outgoing[None], (devices_req,) + outgoing.shape),
        "req",
        split_axis=0,
        concat_axis=0,
        tiled=True,
    ).reshape(total_rows, outgoing.shape[1])
    normed_all = gathered[:, :width_local]
    fresh_all = gathered[:, width_local:].reshape(total_rows, kv_local, channels)
    ffn_width = w_gate.shape[1]
    joined = jnp.concatenate([w_gate, w_up], axis=1)
    partial_both = jnp.dot(normed_all, joined, preferred_element_type=jnp.float32)
    group_rows = total_rows // devices_kvh
    summed = jnp.sum(
        lax.all_to_all(
            partial_both.reshape(devices_kvh, group_rows, 2 * ffn_width),
            "kvh",
            split_axis=0,
            concat_axis=0,
            tiled=True,
        ),
        axis=0,
    )
    hidden_part = (jax.nn.silu(summed[:, :ffn_width]) * summed[:, ffn_width:]).astype(
        jnp.bfloat16
    )
    hidden = lax.all_to_all(
        jnp.broadcast_to(hidden_part[None], (devices_kvh,) + hidden_part.shape),
        "kvh",
        split_axis=0,
        concat_axis=0,
        tiled=True,
    ).reshape(total_rows, ffn_width)
    lowered_parts = jnp.dot(hidden, w_down, preferred_element_type=jnp.float32)
    lowered = jnp.sum(
        lax.all_to_all(
            lowered_parts.reshape(devices_req, row_count, width_local),
            "req",
            split_axis=0,
            concat_axis=0,
            tiled=True,
        ),
        axis=0,
    )
    result = (residual_wide + lowered).astype(jnp.bfloat16)

    arrived = received[source_owner]
    new_blocks = mask_blocks(arrived, lengths[arriving], fresh_all[arriving])
    new_pool = new_blocks.reshape(row_count * pages_per, kv_local, page_len, channels)
    return (result, new_pool)


def solution(mesh):
    in_specs = (
        P("req", "kvh"),
        P(),
        P(None, "kvh"),
        P(None, "kvh"),
        P(None, "kvh"),
        P(),
        P(),
        P("kvh", None),
        P("kvh"),
        P("kvh", "req"),
        P("kvh", "req"),
        P("req", "kvh"),
        P("req", "kvh", None, None),
        P(),
        P("req", None),
        P(),
    )
    out_specs = (P("req", "kvh"), P("req", "kvh", None, None))
    return jax.shard_map(
        per_device, mesh=mesh, in_specs=in_specs, out_specs=out_specs, check_vma=False
    )
```

```python
import math

import jax
import jax.numpy as jnp
from jax import lax
from jax.sharding import PartitionSpec as P

D = 2560


EPSILON = 1e-06


def rms_norm(values, norm_gain):
    mean_sq = jnp.mean(values * values, axis=-1, keepdims=True)
    return values * lax.rsqrt(mean_sq + EPSILON) * norm_gain


def rotary(values, positions):
    half_dim = values.shape[-1] // 2
    frequency = jnp.exp(
        jnp.arange(half_dim, dtype=jnp.float32) * (-2.0 * math.log(1000000.0) / values.shape[-1])
    )
    angles = positions.astype(jnp.float32)[:, None, None] * frequency
    cosine = jnp.cos(angles)
    sine_part = jnp.sin(angles)
    first_half = values[..., :half_dim]
    second_half = values[..., half_dim:]
    return jnp.concatenate(
        [
            first_half * cosine - second_half * sine_part,
            second_half * cosine + first_half * sine_part,
        ],
        axis=-1,
    )


def mask_blocks(blocks, lengths_now, fresh):
    row_count, pages_per, kv_local, page_len, channels = blocks.shape
    positions = (
        jnp.arange(pages_per, dtype=jnp.int32)[:, None] * page_len
        + jnp.arange(page_len, dtype=jnp.int32)[None, :]
    )
    positions = positions[None, :, None, :, None]
    lengths_col = lengths_now[:, None, None, None, None]
    kept = positions < lengths_col
    placed = positions == lengths_col
    return jnp.where(
        kept,
        blocks,
        jnp.where(placed, fresh[:, None, :, None, :], jnp.zeros((), jnp.bfloat16)),
    )


def attend(query, sequence, lengths_now):
    row_count, kv_local, span_len, channels = sequence.shape
    head_dim = channels // 2
    q_local = query.shape[1]
    group_size = q_local // kv_local
    grouped = query.reshape(row_count, kv_local, group_size, head_dim)
    scores = jnp.einsum(
        "rkgd,rktd->rkgt", grouped, sequence[..., :head_dim], preferred_element_type=jnp.float32
    ) * (1.0 / math.sqrt(head_dim))
    positions = jnp.arange(span_len, dtype=jnp.int32)
    valid = positions[None, None, None, :] <= lengths_now[:, None, None, None]
    scores = jnp.where(valid, scores, -jnp.inf)
    weights = jax.nn.softmax(scores, axis=-1).astype(jnp.bfloat16)
    mixed = jnp.einsum(
        "rkgt,rktd->rkgd", weights, sequence[..., head_dim:], preferred_element_type=jnp.float32
    )
    return mixed.reshape(row_count, q_local * head_dim).astype(jnp.bfloat16)


def per_device(
    states,
    attn_gain,
    w_query,
    w_key,
    w_value,
    query_gain,
    key_gain,
    w_output,
    ffn_gain,
    w_gate,
    w_up,
    w_down,
    kv_pool,
    lengths,
    page_table,
    new_order,
):
    devices_req = lax.axis_size("req")
    my_index = lax.axis_index("req")
    kvh_index = lax.axis_index("kvh")
    row_count = states.shape[0]
    width_local = states.shape[1]
    head_dim = query_gain.shape[0]
    kv_local = w_key.shape[1] // head_dim
    q_local = w_query.shape[1] // head_dim
    pages_per = page_table.shape[1]
    page_len = kv_pool.shape[2]
    channels = 2 * head_dim
    total_rows = new_order.shape[0]

    home = my_index * row_count + jnp.arange(row_count, dtype=jnp.int32)
    new_slot = jnp.argmax((new_order[None, :] == home[:, None]).astype(jnp.int32), axis=1)
    destination = new_slot // row_count
    peer_ids = jnp.arange(devices_req, dtype=jnp.int32)
    matches = destination[None, :] == peer_ids[:, None]
    picked = jnp.argmax(matches.astype(jnp.int32), axis=1)
    picked_pages = page_table[picked]
    first_pages = pages_per // 2
    parcels_first = kv_pool[picked_pages[:, :first_pages]]
    received_first = lax.all_to_all(
        parcels_first, "req", split_axis=0, concat_axis=0, tiled=True
    )
    parcels_second = kv_pool[picked_pages[:, first_pages:]]
    page_block = kv_local * page_len * channels
    second_pages_flat = (pages_per - first_pages) * page_block
    arriving = lax.dynamic_slice_in_dim(new_order, my_index * row_count, row_count)
    source_owner = arriving // row_count

    full_states = lax.all_gather(states, "kvh", axis=1, tiled=True)
    normed = rms_norm(full_states.astype(jnp.float32), attn_gain.astype(jnp.float32)).astype(
        jnp.bfloat16
    )
    query = jnp.dot(normed, w_query, preferred_element_type=jnp.float32).reshape(
        row_count, q_local, head_dim
    )
    key_new = jnp.dot(normed, w_key, preferred_element_type=jnp.float32).reshape(
        row_count, kv_local, head_dim
    )
    value_new = jnp.dot(normed, w_value, preferred_element_type=jnp.float32).reshape(
        row_count, kv_local, head_dim
    )
    positions_home = lengths[home]
    query = rotary(rms_norm(query, query_gain.astype(jnp.float32)), positions_home).astype(
        jnp.bfloat16
    )
    key_new = rotary(rms_norm(key_new, key_gain.astype(jnp.float32)), positions_home).astype(
        jnp.bfloat16
    )
    fresh = jnp.concatenate([key_new, value_new.astype(jnp.bfloat16)], axis=-1)
    home_blocks = mask_blocks(kv_pool[page_table], positions_home, fresh)
    sequence = home_blocks.transpose(0, 2, 1, 3, 4).reshape(
        row_count, kv_local, pages_per * page_len, channels
    )
    mixed = attend(query, sequence, positions_home)
    partial_out = jnp.dot(mixed, w_output, preferred_element_type=jnp.float32)
    devices_kvh = lax.axis_size("kvh")
    attn_out = partial_out
    step = 1
    while step < devices_kvh:
        attn_out = attn_out + lax.ppermute(
            attn_out, "kvh", [(i, i ^ step) for i in range(devices_kvh)]
        )
        step *= 2
    residual_full = (full_states.astype(jnp.float32) + attn_out).astype(jnp.bfloat16)
    residual_wide_full = residual_full.astype(jnp.float32)
    total_sq = jnp.sum(residual_wide_full * residual_wide_full, axis=-1, keepdims=True)
    residual_wide = lax.dynamic_slice_in_dim(
        residual_wide_full, kvh_index * width_local, width_local, axis=1
    )
    normed_two = (
        residual_wide * lax.rsqrt(total_sq / D + EPSILON) * ffn_gain.astype(jnp.float32)
    ).astype(jnp.bfloat16)

    fresh_flat = fresh.reshape(row_count, kv_local * channels)
    outgoing = jnp.concatenate([normed_two, fresh_flat], axis=1)
    outgoing_width = outgoing.shape[1]
    second_buffer = jnp.concatenate(
        [
            parcels_second.reshape(devices_req, second_pages_flat),
            jnp.zeros((devices_req, row_count * outgoing_width), jnp.bfloat16),
        ],
        axis=1,
    )
    received_first, second_buffer = lax.optimization_barrier((received_first, second_buffer))
    second_buffer = lax.dynamic_update_slice(
        second_buffer,
        jnp.broadcast_to(
            outgoing.reshape(1, row_count * outgoing_width),
            (devices_req, row_count * outgoing_width),
        ),
        (0, second_pages_flat),
    )
    received_second = lax.all_to_all(
        second_buffer, "req", split_axis=0, concat_axis=0, tiled=True
    )
    gathered = received_second[:, second_pages_flat:].reshape(total_rows, outgoing_width)
    received = jnp.concatenate(
        [
            received_first,
            received_second[:, :second_pages_flat].reshape(
                (devices_req, pages_per - first_pages) + parcels_second.shape[2:]
            ),
        ],
        axis=1,
    )
    normed_all = gathered[:, :width_local]
    fresh_all = gathered[:, width_local:].reshape(total_rows, kv_local, channels)
    ffn_width = w_gate.shape[1]
    joined = jnp.concatenate([w_gate, w_up], axis=1)
    partial_both = jnp.dot(normed_all, joined, preferred_element_type=jnp.float32)
    group_rows = total_rows // devices_kvh
    summed = jnp.sum(
        lax.all_to_all(
            partial_both.reshape(devices_kvh, group_rows, 2 * ffn_width),
            "kvh",
            split_axis=0,
            concat_axis=0,
            tiled=True,
        ),
        axis=0,
    )
    hidden_part = (jax.nn.silu(summed[:, :ffn_width]) * summed[:, ffn_width:]).astype(
        jnp.bfloat16
    )
    hidden = lax.all_to_all(
        jnp.broadcast_to(hidden_part[None], (devices_kvh,) + hidden_part.shape),
        "kvh",
        split_axis=0,
        concat_axis=0,
        tiled=True,
    ).reshape(total_rows, ffn_width)
    lowered_parts = jnp.dot(hidden, w_down, preferred_element_type=jnp.float32)
    lowered = jnp.sum(
        lax.all_to_all(
            lowered_parts.reshape(devices_req, row_count, width_local),
            "req",
            split_axis=0,
            concat_axis=0,
            tiled=True,
        ),
        axis=0,
    )
    result = (residual_wide + lowered).astype(jnp.bfloat16)

    arrived = received[source_owner]
    new_blocks = mask_blocks(arrived, lengths[arriving], fresh_all[arriving])
    new_pool = new_blocks.reshape(row_count * pages_per, kv_local, page_len, channels)
    return (result, new_pool)


def solution(mesh):
    in_specs = (
        P("req", "kvh"),
        P(),
        P(None, "kvh"),
        P(None, "kvh"),
        P(None, "kvh"),
        P(),
        P(),
        P("kvh", None),
        P("kvh"),
        P("kvh", "req"),
        P("kvh", "req"),
        P("req", "kvh"),
        P("req", "kvh", None, None),
        P(),
        P("req", None),
        P(),
    )
    out_specs = (P("req", "kvh"), P("req", "kvh", None, None))
    return jax.shard_map(
        per_device, mesh=mesh, in_specs=in_specs, out_specs=out_specs, check_vma=False
    )
```

```python
import math

import jax
import jax.numpy as jnp
from jax import lax
from jax.sharding import PartitionSpec as P

D = 2560


EPSILON = 1e-06


def rms_norm(values, norm_gain):
    mean_sq = jnp.mean(values * values, axis=-1, keepdims=True)
    return values * lax.rsqrt(mean_sq + EPSILON) * norm_gain


def rotary(values, positions):
    half_dim = values.shape[-1] // 2
    frequency = jnp.exp(
        jnp.arange(half_dim, dtype=jnp.float32) * (-2.0 * math.log(1000000.0) / values.shape[-1])
    )
    angles = positions.astype(jnp.float32)[:, None, None] * frequency
    cosine = jnp.cos(angles)
    sine_part = jnp.sin(angles)
    first_half = values[..., :half_dim]
    second_half = values[..., half_dim:]
    return jnp.concatenate(
        [
            first_half * cosine - second_half * sine_part,
            second_half * cosine + first_half * sine_part,
        ],
        axis=-1,
    )


def mask_blocks(blocks, lengths_now, fresh, first_page=0):
    row_count, pages_per, kv_local, page_len, channels = blocks.shape
    positions = (
        (first_page + jnp.arange(pages_per, dtype=jnp.int32))[:, None] * page_len
        + jnp.arange(page_len, dtype=jnp.int32)[None, :]
    )
    positions = positions[None, :, None, :, None]
    lengths_col = lengths_now[:, None, None, None, None]
    kept = positions < lengths_col
    placed = positions == lengths_col
    return jnp.where(
        kept,
        blocks,
        jnp.where(placed, fresh[:, None, :, None, :], jnp.zeros((), jnp.bfloat16)),
    )


def attend(query, sequence, lengths_now):
    row_count, kv_local, span_len, channels = sequence.shape
    head_dim = channels // 2
    q_local = query.shape[1]
    group_size = q_local // kv_local
    grouped = query.reshape(row_count, kv_local, group_size, head_dim)
    scores = jnp.einsum(
        "rkgd,rktd->rkgt", grouped, sequence[..., :head_dim], preferred_element_type=jnp.float32
    ) * (1.0 / math.sqrt(head_dim))
    positions = jnp.arange(span_len, dtype=jnp.int32)
    valid = positions[None, None, None, :] <= lengths_now[:, None, None, None]
    scores = jnp.where(valid, scores, -jnp.inf)
    weights = jax.nn.softmax(scores, axis=-1).astype(jnp.bfloat16)
    mixed = jnp.einsum(
        "rkgt,rktd->rkgd", weights, sequence[..., head_dim:], preferred_element_type=jnp.float32
    )
    return mixed.reshape(row_count, q_local * head_dim).astype(jnp.bfloat16)


def per_device(
    states,
    attn_gain,
    w_query,
    w_key,
    w_value,
    query_gain,
    key_gain,
    w_output,
    ffn_gain,
    w_gate,
    w_up,
    w_down,
    kv_pool,
    lengths,
    page_table,
    new_order,
):
    devices_req = lax.axis_size("req")
    my_index = lax.axis_index("req")
    kvh_index = lax.axis_index("kvh")
    row_count = states.shape[0]
    width_local = states.shape[1]
    head_dim = query_gain.shape[0]
    kv_local = w_key.shape[1] // head_dim
    q_local = w_query.shape[1] // head_dim
    pages_per = page_table.shape[1]
    page_len = kv_pool.shape[2]
    channels = 2 * head_dim
    total_rows = new_order.shape[0]

    home = my_index * row_count + jnp.arange(row_count, dtype=jnp.int32)
    new_slot = jnp.argmax((new_order[None, :] == home[:, None]).astype(jnp.int32), axis=1)
    destination = new_slot // row_count
    peer_ids = jnp.arange(devices_req, dtype=jnp.int32)
    matches = destination[None, :] == peer_ids[:, None]
    picked = jnp.argmax(matches.astype(jnp.int32), axis=1)
    picked_pages = page_table[picked]
    first_pages = pages_per // 2
    second_pages = pages_per - first_pages
    parcels_first = kv_pool[picked_pages[:, :first_pages]]
    received_first = lax.all_to_all(
        parcels_first, "req", split_axis=0, concat_axis=0, tiled=True
    )
    second_span = second_pages * page_len
    parcels_second = kv_pool[picked_pages[:, first_pages:]].reshape(
        devices_req, second_span, channels
    )
    arriving = lax.dynamic_slice_in_dim(new_order, my_index * row_count, row_count)
    source_owner = arriving // row_count

    full_states = lax.all_gather(states, "kvh", axis=1, tiled=True)
    normed = rms_norm(full_states.astype(jnp.float32), attn_gain.astype(jnp.float32)).astype(
        jnp.bfloat16
    )
    query = jnp.dot(normed, w_query, preferred_element_type=jnp.float32).reshape(
        row_count, q_local, head_dim
    )
    key_new = jnp.dot(normed, w_key, preferred_element_type=jnp.float32).reshape(
        row_count, kv_local, head_dim
    )
    value_new = jnp.dot(normed, w_value, preferred_element_type=jnp.float32).reshape(
        row_count, kv_local, head_dim
    )
    positions_home = lengths[home]
    query = rotary(rms_norm(query, query_gain.astype(jnp.float32)), positions_home).astype(
        jnp.bfloat16
    )
    key_new = rotary(rms_norm(key_new, key_gain.astype(jnp.float32)), positions_home).astype(
        jnp.bfloat16
    )
    fresh = jnp.concatenate([key_new, value_new.astype(jnp.bfloat16)], axis=-1)
    home_blocks = mask_blocks(kv_pool[page_table], positions_home, fresh)
    sequence = home_blocks.transpose(0, 2, 1, 3, 4).reshape(
        row_count, kv_local, pages_per * page_len, channels
    )
    mixed = attend(query, sequence, positions_home)
    partial_out = jnp.dot(mixed, w_output, preferred_element_type=jnp.float32)
    devices_kvh = lax.axis_size("kvh")
    attn_out = partial_out
    step = 1
    while step < devices_kvh:
        attn_out = attn_out + lax.ppermute(
            attn_out, "kvh", [(i, i ^ step) for i in range(devices_kvh)]
        )
        step *= 2
    residual_full = (full_states.astype(jnp.float32) + attn_out).astype(jnp.bfloat16)
    residual_wide_full = residual_full.astype(jnp.float32)
    total_sq = jnp.sum(residual_wide_full * residual_wide_full, axis=-1, keepdims=True)
    residual_wide = lax.dynamic_slice_in_dim(
        residual_wide_full, kvh_index * width_local, width_local, axis=1
    )
    normed_two = (
        residual_wide * lax.rsqrt(total_sq / D + EPSILON) * ffn_gain.astype(jnp.float32)
    ).astype(jnp.bfloat16)

    fresh_flat = fresh.reshape(row_count, kv_local * channels)
    outgoing = jnp.concatenate([normed_two, fresh_flat], axis=1)
    outgoing_width = outgoing.shape[1]
    extra_rows = -(-(row_count * outgoing_width) // channels)
    extra_padded = -(-extra_rows // 32) * 32
    second_buffer = jnp.concatenate(
        [parcels_second, jnp.zeros((devices_req, extra_padded, channels), jnp.bfloat16)],
        axis=1,
    )
    received_first, second_buffer = lax.optimization_barrier((received_first, second_buffer))
    extra = jnp.pad(
        outgoing.reshape(row_count * outgoing_width),
        (0, extra_padded * channels - row_count * outgoing_width),
    ).reshape(1, extra_padded, channels)
    second_buffer = lax.dynamic_update_slice(
        second_buffer,
        jnp.broadcast_to(extra, (devices_req, extra_padded, channels)),
        (0, second_span, 0),
    )
    received_second = lax.all_to_all(
        second_buffer, "req", split_axis=0, concat_axis=0, tiled=True
    )
    gathered = (
        received_second[:, second_span:, :]
        .reshape(devices_req, extra_padded * channels)[:, : row_count * outgoing_width]
        .reshape(total_rows, outgoing_width)
    )
    normed_all = gathered[:, :width_local]
    fresh_all = gathered[:, width_local:].reshape(total_rows, kv_local, channels)
    ffn_width = w_gate.shape[1]
    joined = jnp.concatenate([w_gate, w_up], axis=1)
    partial_both = jnp.dot(normed_all, joined, preferred_element_type=jnp.float32)
    group_rows = total_rows // devices_kvh
    summed = jnp.sum(
        lax.all_to_all(
            partial_both.reshape(devices_kvh, group_rows, 2 * ffn_width),
            "kvh",
            split_axis=0,
            concat_axis=0,
            tiled=True,
        ),
        axis=0,
    )
    hidden_part = (jax.nn.silu(summed[:, :ffn_width]) * summed[:, ffn_width:]).astype(
        jnp.bfloat16
    )
    hidden = lax.all_to_all(
        jnp.broadcast_to(hidden_part[None], (devices_kvh,) + hidden_part.shape),
        "kvh",
        split_axis=0,
        concat_axis=0,
        tiled=True,
    ).reshape(total_rows, ffn_width)
    lowered_parts = jnp.dot(hidden, w_down, preferred_element_type=jnp.float32)
    lowered = jnp.sum(
        lax.all_to_all(
            lowered_parts.reshape(devices_req, row_count, width_local),
            "req",
            split_axis=0,
            concat_axis=0,
            tiled=True,
        ),
        axis=0,
    )
    result = (residual_wide + lowered).astype(jnp.bfloat16)

    lengths_new = lengths[arriving]
    fresh_new = fresh_all[arriving]
    blocks_first = mask_blocks(received_first[source_owner], lengths_new, fresh_new, 0)
    blocks_second = mask_blocks(
        received_second[:, :second_span, :]
        .reshape(devices_req, second_pages, kv_local, page_len, channels)[source_owner],
        lengths_new,
        fresh_new,
        first_pages,
    )
    new_blocks = jnp.concatenate([blocks_first, blocks_second], axis=1)
    new_pool = new_blocks.reshape(row_count * pages_per, kv_local, page_len, channels)
    return (result, new_pool)


def solution(mesh):
    in_specs = (
        P("req", "kvh"),
        P(),
        P(None, "kvh"),
        P(None, "kvh"),
        P(None, "kvh"),
        P(),
        P(),
        P("kvh", None),
        P("kvh"),
        P("kvh", "req"),
        P("kvh", "req"),
        P("req", "kvh"),
        P("req", "kvh", None, None),
        P(),
        P("req", None),
        P(),
    )
    out_specs = (P("req", "kvh"), P("req", "kvh", None, None))
    return jax.shard_map(
        per_device, mesh=mesh, in_specs=in_specs, out_specs=out_specs, check_vma=False
    )
```

```python
import math

import jax
import jax.numpy as jnp
from jax import lax
from jax.sharding import PartitionSpec as P

D = 2560


EPSILON = 1e-06


def rms_norm(values, norm_gain):
    mean_sq = jnp.mean(values * values, axis=-1, keepdims=True)
    return values * lax.rsqrt(mean_sq + EPSILON) * norm_gain


def rotary(values, positions):
    half_dim = values.shape[-1] // 2
    frequency = jnp.exp(
        jnp.arange(half_dim, dtype=jnp.float32) * (-2.0 * math.log(1000000.0) / values.shape[-1])
    )
    angles = positions.astype(jnp.float32)[:, None, None] * frequency
    cosine = jnp.cos(angles)
    sine_part = jnp.sin(angles)
    first_half = values[..., :half_dim]
    second_half = values[..., half_dim:]
    return jnp.concatenate(
        [
            first_half * cosine - second_half * sine_part,
            second_half * cosine + first_half * sine_part,
        ],
        axis=-1,
    )


def mask_blocks(blocks, lengths_now, fresh, first_page=0):
    row_count, pages_per, kv_local, page_len, channels = blocks.shape
    positions = (
        (first_page + jnp.arange(pages_per, dtype=jnp.int32))[:, None] * page_len
        + jnp.arange(page_len, dtype=jnp.int32)[None, :]
    )
    positions = positions[None, :, None, :, None]
    lengths_col = lengths_now[:, None, None, None, None]
    kept = positions < lengths_col
    placed = positions == lengths_col
    return jnp.where(
        kept,
        blocks,
        jnp.where(placed, fresh[:, None, :, None, :], jnp.zeros((), jnp.bfloat16)),
    )


def attend(query, sequence, lengths_now):
    row_count, kv_local, span_len, channels = sequence.shape
    head_dim = channels // 2
    q_local = query.shape[1]
    group_size = q_local // kv_local
    grouped = query.reshape(row_count, kv_local, group_size, head_dim)
    scores = jnp.einsum(
        "rkgd,rktd->rkgt", grouped, sequence[..., :head_dim], preferred_element_type=jnp.float32
    ) * (1.0 / math.sqrt(head_dim))
    positions = jnp.arange(span_len, dtype=jnp.int32)
    valid = positions[None, None, None, :] <= lengths_now[:, None, None, None]
    scores = jnp.where(valid, scores, -jnp.inf)
    weights = jax.nn.softmax(scores, axis=-1).astype(jnp.bfloat16)
    mixed = jnp.einsum(
        "rkgt,rktd->rkgd", weights, sequence[..., head_dim:], preferred_element_type=jnp.float32
    )
    return mixed.reshape(row_count, q_local * head_dim).astype(jnp.bfloat16)


def per_device(
    states,
    attn_gain,
    w_query,
    w_key,
    w_value,
    query_gain,
    key_gain,
    w_output,
    ffn_gain,
    w_gate,
    w_up,
    w_down,
    kv_pool,
    lengths,
    page_table,
    new_order,
):
    devices_req = lax.axis_size("req")
    my_index = lax.axis_index("req")
    kvh_index = lax.axis_index("kvh")
    row_count = states.shape[0]
    width_local = states.shape[1]
    head_dim = query_gain.shape[0]
    kv_local = w_key.shape[1] // head_dim
    q_local = w_query.shape[1] // head_dim
    pages_per = page_table.shape[1]
    page_len = kv_pool.shape[2]
    channels = 2 * head_dim
    total_rows = new_order.shape[0]

    home = my_index * row_count + jnp.arange(row_count, dtype=jnp.int32)
    new_slot = jnp.argmax((new_order[None, :] == home[:, None]).astype(jnp.int32), axis=1)
    destination = new_slot // row_count
    peer_ids = jnp.arange(devices_req, dtype=jnp.int32)
    matches = destination[None, :] == peer_ids[:, None]
    picked = jnp.argmax(matches.astype(jnp.int32), axis=1)
    picked_pages = page_table[picked]
    first_pages = pages_per // 2
    second_pages = pages_per - first_pages
    parcels_first = kv_pool[picked_pages[:, :first_pages]]
    received_first = lax.all_to_all(
        parcels_first, "req", split_axis=0, concat_axis=0, tiled=True
    )
    second_span = second_pages * page_len
    parcels_second = kv_pool[picked_pages[:, first_pages:]].reshape(
        devices_req, second_span, channels
    )
    arriving = lax.dynamic_slice_in_dim(new_order, my_index * row_count, row_count)
    source_owner = arriving // row_count

    full_states = lax.all_gather(states, "kvh", axis=1, tiled=True)
    normed = rms_norm(full_states.astype(jnp.float32), attn_gain.astype(jnp.float32)).astype(
        jnp.bfloat16
    )
    query = jnp.dot(normed, w_query, preferred_element_type=jnp.float32).reshape(
        row_count, q_local, head_dim
    )
    key_new = jnp.dot(normed, w_key, preferred_element_type=jnp.float32).reshape(
        row_count, kv_local, head_dim
    )
    value_new = jnp.dot(normed, w_value, preferred_element_type=jnp.float32).reshape(
        row_count, kv_local, head_dim
    )
    positions_home = lengths[home]
    query = rotary(rms_norm(query, query_gain.astype(jnp.float32)), positions_home).astype(
        jnp.bfloat16
    )
    key_new = rotary(rms_norm(key_new, key_gain.astype(jnp.float32)), positions_home).astype(
        jnp.bfloat16
    )
    fresh = jnp.concatenate([key_new, value_new.astype(jnp.bfloat16)], axis=-1)
    home_blocks = mask_blocks(kv_pool[page_table], positions_home, fresh)
    sequence = home_blocks.transpose(0, 2, 1, 3, 4).reshape(
        row_count, kv_local, pages_per * page_len, channels
    )
    mixed = attend(query, sequence, positions_home)
    partial_out = jnp.dot(mixed, w_output, preferred_element_type=jnp.float32)
    devices_kvh = lax.axis_size("kvh")
    attn_out = partial_out
    step = 1
    while step < devices_kvh:
        attn_out = attn_out + lax.ppermute(
            attn_out, "kvh", [(i, i ^ step) for i in range(devices_kvh)]
        )
        step *= 2
    residual_full = (full_states.astype(jnp.float32) + attn_out).astype(jnp.bfloat16)
    residual_wide_full = residual_full.astype(jnp.float32)
    total_sq = jnp.sum(residual_wide_full * residual_wide_full, axis=-1, keepdims=True)
    residual_wide = lax.dynamic_slice_in_dim(
        residual_wide_full, kvh_index * width_local, width_local, axis=1
    )
    normed_two = (
        residual_wide * lax.rsqrt(total_sq / D + EPSILON) * ffn_gain.astype(jnp.float32)
    ).astype(jnp.bfloat16)

    fresh_flat = fresh.reshape(row_count, kv_local * channels)
    outgoing = jnp.concatenate([normed_two, fresh_flat], axis=1)
    outgoing_width = outgoing.shape[1]
    extra_rows = -(-(row_count * outgoing_width) // channels)
    extra_padded = -(-extra_rows // 32) * 32
    second_buffer = jnp.concatenate(
        [parcels_second, jnp.zeros((devices_req, extra_padded, channels), jnp.bfloat16)],
        axis=1,
    )
    received_first, second_buffer = lax.optimization_barrier((received_first, second_buffer))
    extra = jnp.pad(
        outgoing.reshape(row_count * outgoing_width),
        (0, extra_padded * channels - row_count * outgoing_width),
    ).reshape(1, extra_padded, channels)
    second_buffer = lax.dynamic_update_slice(
        second_buffer,
        jnp.broadcast_to(extra, (devices_req, extra_padded, channels)),
        (0, second_span, 0),
    )
    received_second = lax.all_to_all(
        second_buffer, "req", split_axis=0, concat_axis=0, tiled=True
    )
    lengths_new = lengths[arriving]
    first_span = first_pages * page_len
    span_first = received_first.reshape(devices_req, first_span, channels)[source_owner]
    span_first = jnp.where(
        jnp.arange(first_span, dtype=jnp.int32)[None, :, None] < lengths_new[:, None, None],
        span_first,
        jnp.zeros((), jnp.bfloat16),
    )
    span_first, received_second = lax.optimization_barrier((span_first, received_second))
    span_second = received_second[source_owner][:, :second_span, :]
    span_second = jnp.where(
        first_span + jnp.arange(second_span, dtype=jnp.int32)[None, :, None]
        < lengths_new[:, None, None],
        span_second,
        jnp.zeros((), jnp.bfloat16),
    )
    gathered = (
        received_second[:, second_span:, :]
        .reshape(devices_req, extra_padded * channels)[:, : row_count * outgoing_width]
        .reshape(total_rows, outgoing_width)
    )
    normed_all = gathered[:, :width_local]
    fresh_all = gathered[:, width_local:].reshape(total_rows, kv_local, channels)
    ffn_width = w_gate.shape[1]
    joined = jnp.concatenate([w_gate, w_up], axis=1)
    partial_both = jnp.dot(normed_all, joined, preferred_element_type=jnp.float32)
    group_rows = total_rows // devices_kvh
    summed = jnp.sum(
        lax.all_to_all(
            partial_both.reshape(devices_kvh, group_rows, 2 * ffn_width),
            "kvh",
            split_axis=0,
            concat_axis=0,
            tiled=True,
        ),
        axis=0,
    )
    hidden_part = (jax.nn.silu(summed[:, :ffn_width]) * summed[:, ffn_width:]).astype(
        jnp.bfloat16
    )
    hidden = lax.all_to_all(
        jnp.broadcast_to(hidden_part[None], (devices_kvh,) + hidden_part.shape),
        "kvh",
        split_axis=0,
        concat_axis=0,
        tiled=True,
    ).reshape(total_rows, ffn_width)
    lowered_parts = jnp.dot(hidden, w_down, preferred_element_type=jnp.float32)
    lowered = jnp.sum(
        lax.all_to_all(
            lowered_parts.reshape(devices_req, row_count, width_local),
            "req",
            split_axis=0,
            concat_axis=0,
            tiled=True,
        ),
        axis=0,
    )
    result = (residual_wide + lowered).astype(jnp.bfloat16)

    new_seq = jnp.concatenate([span_first, span_second], axis=1)
    new_seq = new_seq.at[jnp.arange(row_count), lengths_new].set(
        fresh_all[arriving].reshape(row_count, channels)
    )
    new_pool = new_seq.reshape(row_count * pages_per, kv_local, page_len, channels)
    return (result, new_pool)


def solution(mesh):
    in_specs = (
        P("req", "kvh"),
        P(),
        P(None, "kvh"),
        P(None, "kvh"),
        P(None, "kvh"),
        P(),
        P(),
        P("kvh", None),
        P("kvh"),
        P("kvh", "req"),
        P("kvh", "req"),
        P("req", "kvh"),
        P("req", "kvh", None, None),
        P(),
        P("req", None),
        P(),
    )
    out_specs = (P("req", "kvh"), P("req", "kvh", None, None))
    return jax.shard_map(
        per_device, mesh=mesh, in_specs=in_specs, out_specs=out_specs, check_vma=False
    )
```

```python
import math

import jax
import jax.numpy as jnp
from jax import lax
from jax.sharding import PartitionSpec as P

D = 2560


EPSILON = 1e-06


def rms_norm(values, norm_gain):
    mean_sq = jnp.mean(values * values, axis=-1, keepdims=True)
    return values * lax.rsqrt(mean_sq + EPSILON) * norm_gain


def rotary(values, positions):
    half_dim = values.shape[-1] // 2
    frequency = jnp.exp(
        jnp.arange(half_dim, dtype=jnp.float32) * (-2.0 * math.log(1000000.0) / values.shape[-1])
    )
    angles = positions.astype(jnp.float32)[:, None, None] * frequency
    cosine = jnp.cos(angles)
    sine_part = jnp.sin(angles)
    first_half = values[..., :half_dim]
    second_half = values[..., half_dim:]
    return jnp.concatenate(
        [
            first_half * cosine - second_half * sine_part,
            second_half * cosine + first_half * sine_part,
        ],
        axis=-1,
    )


def mask_blocks(blocks, lengths_now, fresh, first_page=0):
    row_count, pages_per, kv_local, page_len, channels = blocks.shape
    positions = (
        (first_page + jnp.arange(pages_per, dtype=jnp.int32))[:, None] * page_len
        + jnp.arange(page_len, dtype=jnp.int32)[None, :]
    )
    positions = positions[None, :, None, :, None]
    lengths_col = lengths_now[:, None, None, None, None]
    kept = positions < lengths_col
    placed = positions == lengths_col
    return jnp.where(
        kept,
        blocks,
        jnp.where(placed, fresh[:, None, :, None, :], jnp.zeros((), jnp.bfloat16)),
    )


def attend(query, sequence, lengths_now):
    row_count, kv_local, span_len, channels = sequence.shape
    head_dim = channels // 2
    q_local = query.shape[1]
    group_size = q_local // kv_local
    grouped = query.reshape(row_count, kv_local, group_size, head_dim)
    scores = jnp.einsum(
        "rkgd,rktd->rkgt", grouped, sequence[..., :head_dim], preferred_element_type=jnp.float32
    ) * (1.0 / math.sqrt(head_dim))
    positions = jnp.arange(span_len, dtype=jnp.int32)
    valid = positions[None, None, None, :] <= lengths_now[:, None, None, None]
    scores = jnp.where(valid, scores, -jnp.inf)
    weights = jax.nn.softmax(scores, axis=-1).astype(jnp.bfloat16)
    mixed = jnp.einsum(
        "rkgt,rktd->rkgd", weights, sequence[..., head_dim:], preferred_element_type=jnp.float32
    )
    return mixed.reshape(row_count, q_local * head_dim).astype(jnp.bfloat16)


def per_device(
    states,
    attn_gain,
    w_query,
    w_key,
    w_value,
    query_gain,
    key_gain,
    w_output,
    ffn_gain,
    w_gate,
    w_up,
    w_down,
    kv_pool,
    lengths,
    page_table,
    new_order,
):
    devices_req = lax.axis_size("req")
    my_index = lax.axis_index("req")
    kvh_index = lax.axis_index("kvh")
    row_count = states.shape[0]
    width_local = states.shape[1]
    head_dim = query_gain.shape[0]
    kv_local = w_key.shape[1] // head_dim
    q_local = w_query.shape[1] // head_dim
    pages_per = page_table.shape[1]
    page_len = kv_pool.shape[2]
    channels = 2 * head_dim
    total_rows = new_order.shape[0]

    home = my_index * row_count + jnp.arange(row_count, dtype=jnp.int32)
    new_slot = jnp.argmax((new_order[None, :] == home[:, None]).astype(jnp.int32), axis=1)
    destination = new_slot // row_count
    peer_ids = jnp.arange(devices_req, dtype=jnp.int32)
    matches = destination[None, :] == peer_ids[:, None]
    picked = jnp.argmax(matches.astype(jnp.int32), axis=1)
    picked_pages = page_table[picked]
    first_pages = pages_per // 2
    second_pages = pages_per - first_pages
    first_span = first_pages * page_len
    parcels_first = kv_pool[picked_pages[:, :first_pages]].reshape(
        devices_req, first_span, channels
    )
    received_first = lax.all_to_all(
        parcels_first, "req", split_axis=0, concat_axis=0, tiled=True
    )
    second_span = second_pages * page_len
    parcels_second = kv_pool[picked_pages[:, first_pages:]].reshape(
        devices_req, second_span, channels
    )
    arriving = lax.dynamic_slice_in_dim(new_order, my_index * row_count, row_count)
    source_owner = arriving // row_count

    full_states = lax.all_gather(states, "kvh", axis=1, tiled=True)
    normed = rms_norm(full_states.astype(jnp.float32), attn_gain.astype(jnp.float32)).astype(
        jnp.bfloat16
    )
    query = jnp.dot(normed, w_query, preferred_element_type=jnp.float32).reshape(
        row_count, q_local, head_dim
    )
    key_new = jnp.dot(normed, w_key, preferred_element_type=jnp.float32).reshape(
        row_count, kv_local, head_dim
    )
    value_new = jnp.dot(normed, w_value, preferred_element_type=jnp.float32).reshape(
        row_count, kv_local, head_dim
    )
    positions_home = lengths[home]
    query = rotary(rms_norm(query, query_gain.astype(jnp.float32)), positions_home).astype(
        jnp.bfloat16
    )
    key_new = rotary(rms_norm(key_new, key_gain.astype(jnp.float32)), positions_home).astype(
        jnp.bfloat16
    )
    fresh = jnp.concatenate([key_new, value_new.astype(jnp.bfloat16)], axis=-1)
    home_blocks = mask_blocks(kv_pool[page_table], positions_home, fresh)
    sequence = home_blocks.transpose(0, 2, 1, 3, 4).reshape(
        row_count, kv_local, pages_per * page_len, channels
    )
    mixed = attend(query, sequence, positions_home)
    partial_out = jnp.dot(mixed, w_output, preferred_element_type=jnp.float32)
    devices_kvh = lax.axis_size("kvh")
    attn_out = partial_out
    step = 1
    while step < devices_kvh:
        attn_out = attn_out + lax.ppermute(
            attn_out, "kvh", [(i, i ^ step) for i in range(devices_kvh)]
        )
        step *= 2
    residual_full = (full_states.astype(jnp.float32) + attn_out).astype(jnp.bfloat16)
    residual_wide_full = residual_full.astype(jnp.float32)
    total_sq = jnp.sum(residual_wide_full * residual_wide_full, axis=-1, keepdims=True)
    residual_wide = lax.dynamic_slice_in_dim(
        residual_wide_full, kvh_index * width_local, width_local, axis=1
    )
    normed_two = (
        residual_wide * lax.rsqrt(total_sq / D + EPSILON) * ffn_gain.astype(jnp.float32)
    ).astype(jnp.bfloat16)

    fresh_flat = fresh.reshape(row_count, kv_local * channels)
    outgoing = jnp.concatenate([normed_two, fresh_flat], axis=1)
    outgoing_width = outgoing.shape[1]
    extra_rows = -(-(row_count * outgoing_width) // channels)
    extra_padded = -(-extra_rows // 32) * 32
    second_buffer = jnp.concatenate(
        [parcels_second, jnp.zeros((devices_req, extra_padded, channels), jnp.bfloat16)],
        axis=1,
    )
    received_first, second_buffer = lax.optimization_barrier((received_first, second_buffer))
    extra = jnp.pad(
        outgoing.reshape(row_count * outgoing_width),
        (0, extra_padded * channels - row_count * outgoing_width),
    ).reshape(1, extra_padded, channels)
    second_buffer = lax.dynamic_update_slice(
        second_buffer,
        jnp.broadcast_to(extra, (devices_req, extra_padded, channels)),
        (0, second_span, 0),
    )
    received_second = lax.all_to_all(
        second_buffer, "req", split_axis=0, concat_axis=0, tiled=True
    )
    lengths_new = lengths[arriving]
    span_first = jnp.where(
        jnp.arange(first_span, dtype=jnp.int32)[None, :, None] < lengths_new[:, None, None],
        received_first[source_owner],
        jnp.zeros((), jnp.bfloat16),
    )
    span_first = jnp.concatenate(
        [span_first, jnp.zeros((row_count, second_span, channels), jnp.bfloat16)], axis=1
    )
    span_first, received_second = lax.optimization_barrier((span_first, received_second))
    span_second = received_second[source_owner][:, :second_span, :]
    span_second = jnp.where(
        first_span + jnp.arange(second_span, dtype=jnp.int32)[None, :, None]
        < lengths_new[:, None, None],
        span_second,
        jnp.zeros((), jnp.bfloat16),
    )
    gathered = (
        received_second[:, second_span:, :]
        .reshape(devices_req, extra_padded * channels)[:, : row_count * outgoing_width]
        .reshape(total_rows, outgoing_width)
    )
    normed_all = gathered[:, :width_local]
    fresh_all = gathered[:, width_local:].reshape(total_rows, kv_local, channels)
    ffn_width = w_gate.shape[1]
    joined = jnp.concatenate([w_gate, w_up], axis=1)
    partial_both = jnp.dot(normed_all, joined, preferred_element_type=jnp.float32)
    group_rows = total_rows // devices_kvh
    summed = jnp.sum(
        lax.all_to_all(
            partial_both.reshape(devices_kvh, group_rows, 2 * ffn_width),
            "kvh",
            split_axis=0,
            concat_axis=0,
            tiled=True,
        ),
        axis=0,
    )
    hidden_part = (jax.nn.silu(summed[:, :ffn_width]) * summed[:, ffn_width:]).astype(
        jnp.bfloat16
    )
    hidden = lax.all_to_all(
        jnp.broadcast_to(hidden_part[None], (devices_kvh,) + hidden_part.shape),
        "kvh",
        split_axis=0,
        concat_axis=0,
        tiled=True,
    ).reshape(total_rows, ffn_width)
    lowered_parts = jnp.dot(hidden, w_down, preferred_element_type=jnp.float32)
    lowered = jnp.sum(
        lax.all_to_all(
            lowered_parts.reshape(devices_req, row_count, width_local),
            "req",
            split_axis=0,
            concat_axis=0,
            tiled=True,
        ),
        axis=0,
    )
    result = (residual_wide + lowered).astype(jnp.bfloat16)

    new_seq = lax.dynamic_update_slice(span_first, span_second, (0, first_span, 0))
    new_seq = new_seq.at[jnp.arange(row_count), lengths_new].set(
        fresh_all[arriving].reshape(row_count, channels)
    )
    new_pool = new_seq.reshape(row_count * pages_per, kv_local, page_len, channels)
    return (result, new_pool)


def solution(mesh):
    in_specs = (
        P("req", "kvh"),
        P(),
        P(None, "kvh"),
        P(None, "kvh"),
        P(None, "kvh"),
        P(),
        P(),
        P("kvh", None),
        P("kvh"),
        P("kvh", "req"),
        P("kvh", "req"),
        P("req", "kvh"),
        P("req", "kvh", None, None),
        P(),
        P("req", None),
        P(),
    )
    out_specs = (P("req", "kvh"), P("req", "kvh", None, None))
    return jax.shard_map(
        per_device, mesh=mesh, in_specs=in_specs, out_specs=out_specs, check_vma=False
    )
```

```python
import math

import jax
import jax.numpy as jnp
from jax import lax
from jax.sharding import PartitionSpec as P

D = 2560


EPSILON = 1e-06


def rms_norm(values, norm_gain):
    mean_sq = jnp.mean(values * values, axis=-1, keepdims=True)
    return values * lax.rsqrt(mean_sq + EPSILON) * norm_gain


def rotary(values, positions):
    half_dim = values.shape[-1] // 2
    frequency = jnp.exp(
        jnp.arange(half_dim, dtype=jnp.float32) * (-2.0 * math.log(1000000.0) / values.shape[-1])
    )
    angles = positions.astype(jnp.float32)[:, None, None] * frequency
    cosine = jnp.cos(angles)
    sine_part = jnp.sin(angles)
    first_half = values[..., :half_dim]
    second_half = values[..., half_dim:]
    return jnp.concatenate(
        [
            first_half * cosine - second_half * sine_part,
            second_half * cosine + first_half * sine_part,
        ],
        axis=-1,
    )


def mask_blocks(blocks, lengths_now, fresh, first_page=0):
    row_count, pages_per, kv_local, page_len, channels = blocks.shape
    positions = (
        (first_page + jnp.arange(pages_per, dtype=jnp.int32))[:, None] * page_len
        + jnp.arange(page_len, dtype=jnp.int32)[None, :]
    )
    positions = positions[None, :, None, :, None]
    lengths_col = lengths_now[:, None, None, None, None]
    kept = positions < lengths_col
    placed = positions == lengths_col
    return jnp.where(
        kept,
        blocks,
        jnp.where(placed, fresh[:, None, :, None, :], jnp.zeros((), jnp.bfloat16)),
    )


def attend(query, sequence, lengths_now):
    row_count, kv_local, span_len, channels = sequence.shape
    head_dim = channels // 2
    q_local = query.shape[1]
    group_size = q_local // kv_local
    grouped = query.reshape(row_count, kv_local, group_size, head_dim)
    scores = jnp.einsum(
        "rkgd,rktd->rkgt", grouped, sequence[..., :head_dim], preferred_element_type=jnp.float32
    ) * (1.0 / math.sqrt(head_dim))
    positions = jnp.arange(span_len, dtype=jnp.int32)
    valid = positions[None, None, None, :] <= lengths_now[:, None, None, None]
    scores = jnp.where(valid, scores, -jnp.inf)
    weights = jax.nn.softmax(scores, axis=-1).astype(jnp.bfloat16)
    mixed = jnp.einsum(
        "rkgt,rktd->rkgd", weights, sequence[..., head_dim:], preferred_element_type=jnp.float32
    )
    return mixed.reshape(row_count, q_local * head_dim).astype(jnp.bfloat16)


def per_device(
    states,
    attn_gain,
    w_query,
    w_key,
    w_value,
    query_gain,
    key_gain,
    w_output,
    ffn_gain,
    w_gate,
    w_up,
    w_down,
    kv_pool,
    lengths,
    page_table,
    new_order,
):
    devices_req = lax.axis_size("req")
    my_index = lax.axis_index("req")
    kvh_index = lax.axis_index("kvh")
    row_count = states.shape[0]
    width_local = states.shape[1]
    head_dim = query_gain.shape[0]
    kv_local = w_key.shape[1] // head_dim
    q_local = w_query.shape[1] // head_dim
    pages_per = page_table.shape[1]
    page_len = kv_pool.shape[2]
    channels = 2 * head_dim
    total_rows = new_order.shape[0]

    home = my_index * row_count + jnp.arange(row_count, dtype=jnp.int32)
    new_slot = jnp.sum(
        jnp.where(
            new_order[None, :] == home[:, None],
            jnp.arange(total_rows, dtype=jnp.int32)[None, :],
            0,
        ),
        axis=1,
    )
    destination = new_slot // row_count
    peer_ids = jnp.arange(devices_req, dtype=jnp.int32)
    matches = destination[None, :] == peer_ids[:, None]
    picked_pages = jnp.sum(jnp.where(matches[:, :, None], page_table[None, :, :], 0), axis=1)
    first_pages = pages_per // 2
    second_pages = pages_per - first_pages
    first_span = first_pages * page_len
    parcels_first = kv_pool[picked_pages[:, :first_pages]].reshape(
        devices_req, first_span, channels
    )
    received_first = lax.all_to_all(
        parcels_first, "req", split_axis=0, concat_axis=0, tiled=True
    )
    second_span = second_pages * page_len
    parcels_second = kv_pool[picked_pages[:, first_pages:]].reshape(
        devices_req, second_span, channels
    )
    arriving = lax.dynamic_slice_in_dim(new_order, my_index * row_count, row_count)
    source_owner = arriving // row_count

    full_states = lax.all_gather(states, "kvh", axis=1, tiled=True)
    normed = rms_norm(full_states.astype(jnp.float32), attn_gain.astype(jnp.float32)).astype(
        jnp.bfloat16
    )
    query = jnp.dot(normed, w_query, preferred_element_type=jnp.float32).reshape(
        row_count, q_local, head_dim
    )
    key_new = jnp.dot(normed, w_key, preferred_element_type=jnp.float32).reshape(
        row_count, kv_local, head_dim
    )
    value_new = jnp.dot(normed, w_value, preferred_element_type=jnp.float32).reshape(
        row_count, kv_local, head_dim
    )
    positions_home = lengths[home]
    query = rotary(rms_norm(query, query_gain.astype(jnp.float32)), positions_home).astype(
        jnp.bfloat16
    )
    key_new = rotary(rms_norm(key_new, key_gain.astype(jnp.float32)), positions_home).astype(
        jnp.bfloat16
    )
    fresh = jnp.concatenate([key_new, value_new.astype(jnp.bfloat16)], axis=-1)
    home_blocks = mask_blocks(kv_pool[page_table], positions_home, fresh)
    sequence = home_blocks.transpose(0, 2, 1, 3, 4).reshape(
        row_count, kv_local, pages_per * page_len, channels
    )
    mixed = attend(query, sequence, positions_home)
    partial_out = jnp.dot(mixed, w_output, preferred_element_type=jnp.float32)
    devices_kvh = lax.axis_size("kvh")
    attn_out = partial_out
    step = 1
    while step < devices_kvh:
        attn_out = attn_out + lax.ppermute(
            attn_out, "kvh", [(i, i ^ step) for i in range(devices_kvh)]
        )
        step *= 2
    residual_full = (full_states.astype(jnp.float32) + attn_out).astype(jnp.bfloat16)
    residual_wide_full = residual_full.astype(jnp.float32)
    total_sq = jnp.sum(residual_wide_full * residual_wide_full, axis=-1, keepdims=True)
    residual_wide = lax.dynamic_slice_in_dim(
        residual_wide_full, kvh_index * width_local, width_local, axis=1
    )
    normed_two = (
        residual_wide * lax.rsqrt(total_sq / D + EPSILON) * ffn_gain.astype(jnp.float32)
    ).astype(jnp.bfloat16)

    fresh_flat = fresh.reshape(row_count, kv_local * channels)
    outgoing = jnp.concatenate([normed_two, fresh_flat], axis=1)
    outgoing_width = outgoing.shape[1]
    extra_rows = -(-(row_count * outgoing_width) // channels)
    extra_padded = -(-extra_rows // 32) * 32
    second_buffer = jnp.concatenate(
        [parcels_second, jnp.zeros((devices_req, extra_padded, channels), jnp.bfloat16)],
        axis=1,
    )
    received_first, second_buffer = lax.optimization_barrier((received_first, second_buffer))
    extra = jnp.pad(
        outgoing.reshape(row_count * outgoing_width),
        (0, extra_padded * channels - row_count * outgoing_width),
    ).reshape(1, extra_padded, channels)
    second_buffer = lax.dynamic_update_slice(
        second_buffer,
        jnp.broadcast_to(extra, (devices_req, extra_padded, channels)),
        (0, second_span, 0),
    )
    received_second = lax.all_to_all(
        second_buffer, "req", split_axis=0, concat_axis=0, tiled=True
    )
    lengths_new = lengths[arriving]
    span_first = jnp.where(
        jnp.arange(first_span, dtype=jnp.int32)[None, :, None] < lengths_new[:, None, None],
        received_first[source_owner],
        jnp.zeros((), jnp.bfloat16),
    )
    span_first = jnp.concatenate(
        [span_first, jnp.zeros((row_count, second_span, channels), jnp.bfloat16)], axis=1
    )
    span_first, received_second = lax.optimization_barrier((span_first, received_second))
    span_second = received_second[source_owner][:, :second_span, :]
    span_second = jnp.where(
        first_span + jnp.arange(second_span, dtype=jnp.int32)[None, :, None]
        < lengths_new[:, None, None],
        span_second,
        jnp.zeros((), jnp.bfloat16),
    )
    gathered = (
        received_second[:, second_span:, :]
        .reshape(devices_req, extra_padded * channels)[:, : row_count * outgoing_width]
        .reshape(total_rows, outgoing_width)
    )
    normed_all = gathered[:, :width_local]
    fresh_all = gathered[:, width_local:].reshape(total_rows, kv_local, channels)
    ffn_width = w_gate.shape[1]
    joined = jnp.concatenate([w_gate, w_up], axis=1)
    partial_both = jnp.dot(normed_all, joined, preferred_element_type=jnp.float32)
    group_rows = total_rows // devices_kvh
    summed = jnp.sum(
        lax.all_to_all(
            partial_both.astype(jnp.bfloat16).reshape(devices_kvh, group_rows, 2 * ffn_width),
            "kvh",
            split_axis=0,
            concat_axis=0,
            tiled=True,
        ).astype(jnp.float32),
        axis=0,
    )
    hidden_part = (jax.nn.silu(summed[:, :ffn_width]) * summed[:, ffn_width:]).astype(
        jnp.bfloat16
    )
    hidden = lax.all_to_all(
        jnp.broadcast_to(hidden_part[None], (devices_kvh,) + hidden_part.shape),
        "kvh",
        split_axis=0,
        concat_axis=0,
        tiled=True,
    ).reshape(total_rows, ffn_width)
    lowered_parts = jnp.dot(hidden, w_down, preferred_element_type=jnp.float32)
    lowered = jnp.sum(
        lax.all_to_all(
            lowered_parts.reshape(devices_req, row_count, width_local),
            "req",
            split_axis=0,
            concat_axis=0,
            tiled=True,
        ),
        axis=0,
    )
    result = (residual_wide + lowered).astype(jnp.bfloat16)

    new_seq = lax.dynamic_update_slice(span_first, span_second, (0, first_span, 0))
    new_seq = new_seq.at[jnp.arange(row_count), lengths_new].set(
        fresh_all[arriving].reshape(row_count, channels)
    )
    new_pool = new_seq.reshape(row_count * pages_per, kv_local, page_len, channels)
    return (result, new_pool)


def solution(mesh):
    in_specs = (
        P("req", "kvh"),
        P(),
        P(None, "kvh"),
        P(None, "kvh"),
        P(None, "kvh"),
        P(),
        P(),
        P("kvh", None),
        P("kvh"),
        P("kvh", "req"),
        P("kvh", "req"),
        P("req", "kvh"),
        P("req", "kvh", None, None),
        P(),
        P("req", None),
        P(),
    )
    out_specs = (P("req", "kvh"), P("req", "kvh", None, None))
    return jax.shard_map(
        per_device, mesh=mesh, in_specs=in_specs, out_specs=out_specs, check_vma=False
    )
```

```python
import math

import jax
import jax.numpy as jnp
from jax import lax
from jax.sharding import PartitionSpec as P

D = 2560


EPSILON = 1e-06


def rms_norm(values, norm_gain):
    mean_sq = jnp.mean(values * values, axis=-1, keepdims=True)
    return values * lax.rsqrt(mean_sq + EPSILON) * norm_gain


def rotary(values, positions):
    half_dim = values.shape[-1] // 2
    frequency = jnp.exp(
        jnp.arange(half_dim, dtype=jnp.float32) * (-2.0 * math.log(1000000.0) / values.shape[-1])
    )
    angles = positions.astype(jnp.float32)[:, None, None] * frequency
    cosine = jnp.cos(angles)
    sine_part = jnp.sin(angles)
    first_half = values[..., :half_dim]
    second_half = values[..., half_dim:]
    return jnp.concatenate(
        [
            first_half * cosine - second_half * sine_part,
            second_half * cosine + first_half * sine_part,
        ],
        axis=-1,
    )


def mask_blocks(blocks, lengths_now, fresh, first_page=0):
    row_count, pages_per, kv_local, page_len, channels = blocks.shape
    positions = (
        (first_page + jnp.arange(pages_per, dtype=jnp.int32))[:, None] * page_len
        + jnp.arange(page_len, dtype=jnp.int32)[None, :]
    )
    positions = positions[None, :, None, :, None]
    lengths_col = lengths_now[:, None, None, None, None]
    kept = positions < lengths_col
    placed = positions == lengths_col
    return jnp.where(
        kept,
        blocks,
        jnp.where(placed, fresh[:, None, :, None, :], jnp.zeros((), jnp.bfloat16)),
    )


def attend(query, sequence, lengths_now):
    row_count, kv_local, span_len, channels = sequence.shape
    head_dim = channels // 2
    q_local = query.shape[1]
    group_size = q_local // kv_local
    grouped = query.reshape(row_count, kv_local, group_size, head_dim)
    scores = jnp.einsum(
        "rkgd,rktd->rkgt", grouped, sequence[..., :head_dim], preferred_element_type=jnp.float32
    ) * (1.0 / math.sqrt(head_dim))
    positions = jnp.arange(span_len, dtype=jnp.int32)
    valid = positions[None, None, None, :] <= lengths_now[:, None, None, None]
    scores = jnp.where(valid, scores, -jnp.inf)
    weights = jax.nn.softmax(scores, axis=-1).astype(jnp.bfloat16)
    mixed = jnp.einsum(
        "rkgt,rktd->rkgd", weights, sequence[..., head_dim:], preferred_element_type=jnp.float32
    )
    return mixed.reshape(row_count, q_local * head_dim).astype(jnp.bfloat16)


def per_device(
    states,
    attn_gain,
    w_query,
    w_key,
    w_value,
    query_gain,
    key_gain,
    w_output,
    ffn_gain,
    w_gate,
    w_up,
    w_down,
    kv_pool,
    lengths,
    page_table,
    new_order,
):
    devices_req = lax.axis_size("req")
    my_index = lax.axis_index("req")
    kvh_index = lax.axis_index("kvh")
    row_count = states.shape[0]
    width_local = states.shape[1]
    head_dim = query_gain.shape[0]
    kv_local = w_key.shape[1] // head_dim
    q_local = w_query.shape[1] // head_dim
    pages_per = page_table.shape[1]
    page_len = kv_pool.shape[2]
    channels = 2 * head_dim
    total_rows = new_order.shape[0]

    home = my_index * row_count + jnp.arange(row_count, dtype=jnp.int32)
    new_slot = jnp.sum(
        jnp.where(
            new_order[None, :] == home[:, None],
            jnp.arange(total_rows, dtype=jnp.int32)[None, :],
            0,
        ),
        axis=1,
    )
    destination = new_slot // row_count
    peer_ids = jnp.arange(devices_req, dtype=jnp.int32)
    matches = destination[None, :] == peer_ids[:, None]
    picked_pages = jnp.sum(jnp.where(matches[:, :, None], page_table[None, :, :], 0), axis=1)
    first_pages = pages_per // 2
    second_pages = pages_per - first_pages
    first_span = first_pages * page_len
    parcels_first = kv_pool[picked_pages[:, :first_pages]].reshape(
        devices_req, first_span, channels
    )
    received_first = lax.all_to_all(
        parcels_first, "req", split_axis=0, concat_axis=0, tiled=True
    )
    second_span = second_pages * page_len
    parcels_second = kv_pool[picked_pages[:, first_pages:]].reshape(
        devices_req, second_span, channels
    )
    arriving = lax.dynamic_slice_in_dim(new_order, my_index * row_count, row_count)
    source_owner = arriving // row_count

    full_states = lax.all_gather(states, "kvh", axis=1, tiled=True)
    normed = rms_norm(full_states.astype(jnp.float32), attn_gain.astype(jnp.float32)).astype(
        jnp.bfloat16
    )
    query = jnp.dot(normed, w_query, preferred_element_type=jnp.float32).reshape(
        row_count, q_local, head_dim
    )
    key_new = jnp.dot(normed, w_key, preferred_element_type=jnp.float32).reshape(
        row_count, kv_local, head_dim
    )
    value_new = jnp.dot(normed, w_value, preferred_element_type=jnp.float32).reshape(
        row_count, kv_local, head_dim
    )
    positions_home = lengths[home]
    query = rotary(rms_norm(query, query_gain.astype(jnp.float32)), positions_home).astype(
        jnp.bfloat16
    )
    key_new = rotary(rms_norm(key_new, key_gain.astype(jnp.float32)), positions_home).astype(
        jnp.bfloat16
    )
    fresh = jnp.concatenate([key_new, value_new.astype(jnp.bfloat16)], axis=-1)
    home_blocks = mask_blocks(kv_pool[page_table], positions_home, fresh)
    sequence = home_blocks.transpose(0, 2, 1, 3, 4).reshape(
        row_count, kv_local, pages_per * page_len, channels
    )
    mixed = attend(query, sequence, positions_home)
    partial_out = jnp.dot(mixed, w_output, preferred_element_type=jnp.float32)
    devices_kvh = lax.axis_size("kvh")
    attn_out = partial_out
    step = 1
    while step < devices_kvh:
        attn_out = attn_out + lax.ppermute(
            attn_out, "kvh", [(i, i ^ step) for i in range(devices_kvh)]
        )
        step *= 2
    residual_full = (full_states.astype(jnp.float32) + attn_out).astype(jnp.bfloat16)
    residual_wide_full = residual_full.astype(jnp.float32)
    total_sq = jnp.sum(residual_wide_full * residual_wide_full, axis=-1, keepdims=True)
    residual_wide = lax.dynamic_slice_in_dim(
        residual_wide_full, kvh_index * width_local, width_local, axis=1
    )
    normed_two = (
        residual_wide * lax.rsqrt(total_sq / D + EPSILON) * ffn_gain.astype(jnp.float32)
    ).astype(jnp.bfloat16)

    fresh_flat = fresh.reshape(row_count, kv_local * channels)
    outgoing = jnp.concatenate([normed_two, fresh_flat], axis=1)
    outgoing_width = outgoing.shape[1]
    received_first, outgoing = lax.optimization_barrier((received_first, outgoing))
    gathered = lax.all_to_all(
        jnp.broadcast_to(outgoing[None], (devices_req,) + outgoing.shape),
        "req",
        split_axis=0,
        concat_axis=0,
        tiled=True,
    ).reshape(total_rows, outgoing_width)
    gathered, parcels_second = lax.optimization_barrier((gathered, parcels_second))
    received_second = lax.all_to_all(
        parcels_second, "req", split_axis=0, concat_axis=0, tiled=True
    )
    lengths_new = lengths[arriving]
    span_first = jnp.where(
        jnp.arange(first_span, dtype=jnp.int32)[None, :, None] < lengths_new[:, None, None],
        received_first[source_owner],
        jnp.zeros((), jnp.bfloat16),
    )
    span_first = jnp.concatenate(
        [span_first, jnp.zeros((row_count, second_span, channels), jnp.bfloat16)], axis=1
    )
    span_first, received_second = lax.optimization_barrier((span_first, received_second))
    span_second = jnp.where(
        first_span + jnp.arange(second_span, dtype=jnp.int32)[None, :, None]
        < lengths_new[:, None, None],
        received_second[source_owner],
        jnp.zeros((), jnp.bfloat16),
    )
    normed_all = gathered[:, :width_local]
    fresh_all = gathered[:, width_local:].reshape(total_rows, kv_local, channels)
    ffn_width = w_gate.shape[1]
    joined = jnp.concatenate([w_gate, w_up], axis=1)
    partial_both = jnp.dot(normed_all, joined, preferred_element_type=jnp.float32)
    group_rows = total_rows // devices_kvh
    current = partial_both.reshape(devices_kvh, group_rows, 2 * ffn_width)
    step = devices_kvh // 2
    while step >= 1:
        upper = (kvh_index // step) % 2 == 1
        half = current.shape[0] // 2
        low, high = current[:half], current[half:]
        keep = jnp.where(upper, high, low)
        send = jnp.where(upper, low, high)
        current = keep + lax.ppermute(
            send, "kvh", [(i, i ^ step) for i in range(devices_kvh)]
        )
        step //= 2
    summed = current[0]
    hidden_part = (jax.nn.silu(summed[:, :ffn_width]) * summed[:, ffn_width:]).astype(
        jnp.bfloat16
    )
    block = hidden_part[None]
    step = 1
    while step < devices_kvh:
        upper = (kvh_index // step) % 2 == 1
        other = lax.ppermute(block, "kvh", [(i, i ^ step) for i in range(devices_kvh)])
        block = jnp.where(
            upper, jnp.concatenate([other, block]), jnp.concatenate([block, other])
        )
        step *= 2
    hidden = block.reshape(total_rows, ffn_width)
    lowered_parts = jnp.dot(hidden, w_down, preferred_element_type=jnp.float32)
    lowered_parts, span_second = lax.optimization_barrier((lowered_parts, span_second))
    lowered = jnp.sum(
        lax.all_to_all(
            lowered_parts.reshape(devices_req, row_count, width_local),
            "req",
            split_axis=0,
            concat_axis=0,
            tiled=True,
        ),
        axis=0,
    )
    result = (residual_wide + lowered).astype(jnp.bfloat16)

    new_seq = lax.dynamic_update_slice(span_first, span_second, (0, first_span, 0))
    new_seq = new_seq.at[jnp.arange(row_count), lengths_new].set(
        fresh_all[arriving].reshape(row_count, channels)
    )
    new_pool = new_seq.reshape(row_count * pages_per, kv_local, page_len, channels)
    return (result, new_pool)


def solution(mesh):
    in_specs = (
        P("req", "kvh"),
        P(),
        P(None, "kvh"),
        P(None, "kvh"),
        P(None, "kvh"),
        P(),
        P(),
        P("kvh", None),
        P("kvh"),
        P("kvh", "req"),
        P("kvh", "req"),
        P("req", "kvh"),
        P("req", "kvh", None, None),
        P(),
        P("req", None),
        P(),
    )
    out_specs = (P("req", "kvh"), P("req", "kvh", None, None))
    return jax.shard_map(
        per_device, mesh=mesh, in_specs=in_specs, out_specs=out_specs, check_vma=False
    )
```

```python
import math

import jax
import jax.numpy as jnp
from jax import lax
from jax.sharding import PartitionSpec as P

D = 2560


EPSILON = 1e-06


def rms_norm(values, norm_gain):
    mean_sq = jnp.mean(values * values, axis=-1, keepdims=True)
    return values * lax.rsqrt(mean_sq + EPSILON) * norm_gain


def rotary(values, positions):
    half_dim = values.shape[-1] // 2
    frequency = jnp.exp(
        jnp.arange(half_dim, dtype=jnp.float32) * (-2.0 * math.log(1000000.0) / values.shape[-1])
    )
    angles = positions.astype(jnp.float32)[:, None, None] * frequency
    cosine = jnp.cos(angles)
    sine_part = jnp.sin(angles)
    first_half = values[..., :half_dim]
    second_half = values[..., half_dim:]
    return jnp.concatenate(
        [
            first_half * cosine - second_half * sine_part,
            second_half * cosine + first_half * sine_part,
        ],
        axis=-1,
    )


def mask_blocks(blocks, lengths_now, fresh, first_page=0):
    row_count, pages_per, kv_local, page_len, channels = blocks.shape
    positions = (
        (first_page + jnp.arange(pages_per, dtype=jnp.int32))[:, None] * page_len
        + jnp.arange(page_len, dtype=jnp.int32)[None, :]
    )
    positions = positions[None, :, None, :, None]
    lengths_col = lengths_now[:, None, None, None, None]
    kept = positions < lengths_col
    placed = positions == lengths_col
    return jnp.where(
        kept,
        blocks,
        jnp.where(placed, fresh[:, None, :, None, :], jnp.zeros((), jnp.bfloat16)),
    )


def attend(query, sequence, lengths_now):
    row_count, kv_local, span_len, channels = sequence.shape
    head_dim = channels // 2
    q_local = query.shape[1]
    group_size = q_local // kv_local
    grouped = query.reshape(row_count, kv_local, group_size, head_dim)
    scores = jnp.einsum(
        "rkgd,rktd->rkgt", grouped, sequence[..., :head_dim], preferred_element_type=jnp.float32
    ) * (1.0 / math.sqrt(head_dim))
    positions = jnp.arange(span_len, dtype=jnp.int32)
    valid = positions[None, None, None, :] <= lengths_now[:, None, None, None]
    scores = jnp.where(valid, scores, -jnp.inf)
    weights = jax.nn.softmax(scores, axis=-1).astype(jnp.bfloat16)
    mixed = jnp.einsum(
        "rkgt,rktd->rkgd", weights, sequence[..., head_dim:], preferred_element_type=jnp.float32
    )
    return mixed.reshape(row_count, q_local * head_dim).astype(jnp.bfloat16)


def per_device(
    states,
    attn_gain,
    w_query,
    w_key,
    w_value,
    query_gain,
    key_gain,
    w_output,
    ffn_gain,
    w_gate,
    w_up,
    w_down,
    kv_pool,
    lengths,
    page_table,
    new_order,
):
    devices_req = lax.axis_size("req")
    my_index = lax.axis_index("req")
    kvh_index = lax.axis_index("kvh")
    row_count = states.shape[0]
    width_local = states.shape[1]
    head_dim = query_gain.shape[0]
    kv_local = w_key.shape[1] // head_dim
    q_local = w_query.shape[1] // head_dim
    pages_per = page_table.shape[1]
    page_len = kv_pool.shape[2]
    channels = 2 * head_dim
    total_rows = new_order.shape[0]

    home = my_index * row_count + jnp.arange(row_count, dtype=jnp.int32)
    new_slot = jnp.sum(
        jnp.where(
            new_order[None, :] == home[:, None],
            jnp.arange(total_rows, dtype=jnp.int32)[None, :],
            0,
        ),
        axis=1,
    )
    destination = new_slot // row_count
    peer_ids = jnp.arange(devices_req, dtype=jnp.int32)
    matches = destination[None, :] == peer_ids[:, None]
    picked_pages = jnp.sum(jnp.where(matches[:, :, None], page_table[None, :, :], 0), axis=1)
    first_pages = pages_per // 2
    second_pages = pages_per - first_pages
    first_span = first_pages * page_len
    parcels_first = kv_pool[picked_pages[:, :first_pages]].reshape(
        devices_req, first_span, channels
    )
    received_first = lax.all_to_all(
        parcels_first, "req", split_axis=0, concat_axis=0, tiled=True
    )
    second_span = second_pages * page_len
    parcels_second = kv_pool[picked_pages[:, first_pages:]].reshape(
        devices_req, second_span, channels
    )
    arriving = lax.dynamic_slice_in_dim(new_order, my_index * row_count, row_count)
    source_owner = arriving // row_count

    full_states = lax.all_gather(states, "kvh", axis=1, tiled=True)
    normed = rms_norm(full_states.astype(jnp.float32), attn_gain.astype(jnp.float32)).astype(
        jnp.bfloat16
    )
    query = jnp.dot(normed, w_query, preferred_element_type=jnp.float32).reshape(
        row_count, q_local, head_dim
    )
    key_new = jnp.dot(normed, w_key, preferred_element_type=jnp.float32).reshape(
        row_count, kv_local, head_dim
    )
    value_new = jnp.dot(normed, w_value, preferred_element_type=jnp.float32).reshape(
        row_count, kv_local, head_dim
    )
    positions_home = lengths[home]
    query = rotary(rms_norm(query, query_gain.astype(jnp.float32)), positions_home).astype(
        jnp.bfloat16
    )
    key_new = rotary(rms_norm(key_new, key_gain.astype(jnp.float32)), positions_home).astype(
        jnp.bfloat16
    )
    fresh = jnp.concatenate([key_new, value_new.astype(jnp.bfloat16)], axis=-1)
    home_blocks = mask_blocks(kv_pool[page_table], positions_home, fresh)
    sequence = home_blocks.transpose(0, 2, 1, 3, 4).reshape(
        row_count, kv_local, pages_per * page_len, channels
    )
    mixed = attend(query, sequence, positions_home)
    partial_out = jnp.dot(mixed, w_output, preferred_element_type=jnp.float32)
    devices_kvh = lax.axis_size("kvh")
    attn_out = partial_out
    step = 1
    while step < devices_kvh:
        attn_out = attn_out + lax.ppermute(
            attn_out, "kvh", [(i, i ^ step) for i in range(devices_kvh)]
        )
        step *= 2
    residual_full = (full_states.astype(jnp.float32) + attn_out).astype(jnp.bfloat16)
    residual_wide_full = residual_full.astype(jnp.float32)
    total_sq = jnp.sum(residual_wide_full * residual_wide_full, axis=-1, keepdims=True)
    residual_wide = lax.dynamic_slice_in_dim(
        residual_wide_full, kvh_index * width_local, width_local, axis=1
    )
    normed_two = (
        residual_wide * lax.rsqrt(total_sq / D + EPSILON) * ffn_gain.astype(jnp.float32)
    ).astype(jnp.bfloat16)

    fresh_flat = fresh.reshape(row_count, kv_local * channels)
    outgoing = jnp.concatenate([normed_two, fresh_flat], axis=1)
    outgoing_width = outgoing.shape[1]
    received_first, outgoing = lax.optimization_barrier((received_first, outgoing))
    gathered = lax.all_to_all(
        jnp.broadcast_to(outgoing[None], (devices_req,) + outgoing.shape),
        "req",
        split_axis=0,
        concat_axis=0,
        tiled=True,
    ).reshape(total_rows, outgoing_width)
    gathered, parcels_second = lax.optimization_barrier((gathered, parcels_second))
    received_second = lax.all_to_all(
        parcels_second, "req", split_axis=0, concat_axis=0, tiled=True
    )
    lengths_new = lengths[arriving]
    span_first = jnp.where(
        jnp.arange(first_span, dtype=jnp.int32)[None, :, None] < lengths_new[:, None, None],
        received_first[source_owner],
        jnp.zeros((), jnp.bfloat16),
    )
    span_first = jnp.concatenate(
        [span_first, jnp.zeros((row_count, second_span, channels), jnp.bfloat16)], axis=1
    )
    span_first, received_second = lax.optimization_barrier((span_first, received_second))
    span_second = jnp.where(
        first_span + jnp.arange(second_span, dtype=jnp.int32)[None, :, None]
        < lengths_new[:, None, None],
        received_second[source_owner],
        jnp.zeros((), jnp.bfloat16),
    )
    normed_all = gathered[:, :width_local]
    fresh_all = gathered[:, width_local:].reshape(total_rows, kv_local, channels)
    ffn_width = w_gate.shape[1]
    joined = jnp.concatenate([w_gate, w_up], axis=1)
    partial_both = jnp.dot(normed_all, joined, preferred_element_type=jnp.float32)
    group_rows = total_rows // devices_kvh
    current = partial_both.reshape(devices_kvh, group_rows, 2 * ffn_width)
    step = devices_kvh // 2
    while step >= 1:
        upper = (kvh_index // step) % 2 == 1
        half = current.shape[0] // 2
        low, high = current[:half], current[half:]
        keep = jnp.where(upper, high, low)
        send = jnp.where(upper, low, high)
        current = keep + lax.ppermute(
            send, "kvh", [(i, i ^ step) for i in range(devices_kvh)]
        )
        step //= 2
    summed = current[0]
    hidden_part = (jax.nn.silu(summed[:, :ffn_width]) * summed[:, ffn_width:]).astype(
        jnp.bfloat16
    )
    block = hidden_part[None]
    step = 1
    while step < devices_kvh:
        upper = (kvh_index // step) % 2 == 1
        other = lax.ppermute(block, "kvh", [(i, i ^ step) for i in range(devices_kvh)])
        block = jnp.where(
            upper, jnp.concatenate([other, block]), jnp.concatenate([block, other])
        )
        step *= 2
    hidden = block.reshape(total_rows, ffn_width)
    lowered_parts = jnp.dot(hidden, w_down, preferred_element_type=jnp.float32)
    lowered_parts, _ = lax.optimization_barrier((lowered_parts, received_second))
    lowered = jnp.sum(
        lax.all_to_all(
            lowered_parts.reshape(devices_req, row_count, width_local),
            "req",
            split_axis=0,
            concat_axis=0,
            tiled=True,
        ),
        axis=0,
    )
    result = (residual_wide + lowered).astype(jnp.bfloat16)

    new_seq = lax.dynamic_update_slice(span_first, span_second, (0, first_span, 0))
    new_seq = new_seq.at[jnp.arange(row_count), lengths_new].set(
        fresh_all[arriving].reshape(row_count, channels)
    )
    new_pool = new_seq.reshape(row_count * pages_per, kv_local, page_len, channels)
    return (result, new_pool)


def solution(mesh):
    in_specs = (
        P("req", "kvh"),
        P(),
        P(None, "kvh"),
        P(None, "kvh"),
        P(None, "kvh"),
        P(),
        P(),
        P("kvh", None),
        P("kvh"),
        P("kvh", "req"),
        P("kvh", "req"),
        P("req", "kvh"),
        P("req", "kvh", None, None),
        P(),
        P("req", None),
        P(),
    )
    out_specs = (P("req", "kvh"), P("req", "kvh", None, None))
    return jax.shard_map(
        per_device, mesh=mesh, in_specs=in_specs, out_specs=out_specs, check_vma=False
    )
```

```python
import math

import jax
import jax.numpy as jnp
from jax import lax
from jax.sharding import PartitionSpec as P

D = 2560


EPSILON = 1e-06


def rms_norm(values, norm_gain):
    mean_sq = jnp.mean(values * values, axis=-1, keepdims=True)
    return values * lax.rsqrt(mean_sq + EPSILON) * norm_gain


def rotary(values, positions):
    half_dim = values.shape[-1] // 2
    frequency = jnp.exp(
        jnp.arange(half_dim, dtype=jnp.float32) * (-2.0 * math.log(1000000.0) / values.shape[-1])
    )
    angles = positions.astype(jnp.float32)[:, None, None] * frequency
    cosine = jnp.cos(angles)
    sine_part = jnp.sin(angles)
    first_half = values[..., :half_dim]
    second_half = values[..., half_dim:]
    return jnp.concatenate(
        [
            first_half * cosine - second_half * sine_part,
            second_half * cosine + first_half * sine_part,
        ],
        axis=-1,
    )


def mask_blocks(blocks, lengths_now, fresh, first_page=0):
    row_count, pages_per, kv_local, page_len, channels = blocks.shape
    positions = (
        (first_page + jnp.arange(pages_per, dtype=jnp.int32))[:, None] * page_len
        + jnp.arange(page_len, dtype=jnp.int32)[None, :]
    )
    positions = positions[None, :, None, :, None]
    lengths_col = lengths_now[:, None, None, None, None]
    kept = positions < lengths_col
    placed = positions == lengths_col
    return jnp.where(
        kept,
        blocks,
        jnp.where(placed, fresh[:, None, :, None, :], jnp.zeros((), jnp.bfloat16)),
    )


def attend(query, sequence, lengths_now):
    row_count, kv_local, span_len, channels = sequence.shape
    head_dim = channels // 2
    q_local = query.shape[1]
    group_size = q_local // kv_local
    grouped = query.reshape(row_count, kv_local, group_size, head_dim)
    scores = jnp.einsum(
        "rkgd,rktd->rkgt", grouped, sequence[..., :head_dim], preferred_element_type=jnp.float32
    ) * (1.0 / math.sqrt(head_dim))
    positions = jnp.arange(span_len, dtype=jnp.int32)
    valid = positions[None, None, None, :] <= lengths_now[:, None, None, None]
    scores = jnp.where(valid, scores, -jnp.inf)
    weights = jax.nn.softmax(scores, axis=-1).astype(jnp.bfloat16)
    mixed = jnp.einsum(
        "rkgt,rktd->rkgd", weights, sequence[..., head_dim:], preferred_element_type=jnp.float32
    )
    return mixed.reshape(row_count, q_local * head_dim).astype(jnp.bfloat16)


def per_device(
    states,
    attn_gain,
    w_query,
    w_key,
    w_value,
    query_gain,
    key_gain,
    w_output,
    ffn_gain,
    w_gate,
    w_up,
    w_down,
    kv_pool,
    lengths,
    page_table,
    new_order,
):
    devices_req = lax.axis_size("req")
    my_index = lax.axis_index("req")
    kvh_index = lax.axis_index("kvh")
    row_count = states.shape[0]
    width_local = states.shape[1]
    head_dim = query_gain.shape[0]
    kv_local = w_key.shape[1] // head_dim
    q_local = w_query.shape[1] // head_dim
    pages_per = page_table.shape[1]
    page_len = kv_pool.shape[2]
    channels = 2 * head_dim
    total_rows = new_order.shape[0]

    home = my_index * row_count + jnp.arange(row_count, dtype=jnp.int32)
    new_slot = jnp.sum(
        jnp.where(
            new_order[None, :] == home[:, None],
            jnp.arange(total_rows, dtype=jnp.int32)[None, :],
            0,
        ),
        axis=1,
    )
    destination = new_slot // row_count
    peer_ids = jnp.arange(devices_req, dtype=jnp.int32)
    matches = destination[None, :] == peer_ids[:, None]
    picked_pages = jnp.sum(jnp.where(matches[:, :, None], page_table[None, :, :], 0), axis=1)
    first_pages = pages_per // 2
    second_pages = pages_per - first_pages
    first_span = first_pages * page_len
    parcels_first = kv_pool[picked_pages[:, :first_pages]].reshape(
        devices_req, first_span, channels
    )
    received_first = lax.all_to_all(
        parcels_first, "req", split_axis=0, concat_axis=0, tiled=True
    )
    second_span = second_pages * page_len
    parcels_second = kv_pool[picked_pages[:, first_pages:]].reshape(
        devices_req, second_span, channels
    )
    arriving = lax.dynamic_slice_in_dim(new_order, my_index * row_count, row_count)
    source_owner = arriving // row_count

    full_states = lax.all_gather(states, "kvh", axis=1, tiled=True)
    normed = rms_norm(full_states.astype(jnp.float32), attn_gain.astype(jnp.float32)).astype(
        jnp.bfloat16
    )
    query = jnp.dot(normed, w_query, preferred_element_type=jnp.float32).reshape(
        row_count, q_local, head_dim
    )
    key_new = jnp.dot(normed, w_key, preferred_element_type=jnp.float32).reshape(
        row_count, kv_local, head_dim
    )
    value_new = jnp.dot(normed, w_value, preferred_element_type=jnp.float32).reshape(
        row_count, kv_local, head_dim
    )
    positions_home = lengths[home]
    query = rotary(rms_norm(query, query_gain.astype(jnp.float32)), positions_home).astype(
        jnp.bfloat16
    )
    key_new = rotary(rms_norm(key_new, key_gain.astype(jnp.float32)), positions_home).astype(
        jnp.bfloat16
    )
    fresh = jnp.concatenate([key_new, value_new.astype(jnp.bfloat16)], axis=-1)
    home_blocks = mask_blocks(kv_pool[page_table], positions_home, fresh)
    sequence = home_blocks.transpose(0, 2, 1, 3, 4).reshape(
        row_count, kv_local, pages_per * page_len, channels
    )
    mixed = attend(query, sequence, positions_home)
    partial_out = jnp.dot(mixed, w_output, preferred_element_type=jnp.float32)
    devices_kvh = lax.axis_size("kvh")
    attn_out = partial_out
    step = 1
    while step < devices_kvh:
        attn_out = attn_out + lax.ppermute(
            attn_out, "kvh", [(i, i ^ step) for i in range(devices_kvh)]
        )
        step *= 2
    residual_full = (full_states.astype(jnp.float32) + attn_out).astype(jnp.bfloat16)
    residual_wide_full = residual_full.astype(jnp.float32)
    total_sq = jnp.sum(residual_wide_full * residual_wide_full, axis=-1, keepdims=True)
    residual_wide = lax.dynamic_slice_in_dim(
        residual_wide_full, kvh_index * width_local, width_local, axis=1
    )
    normed_two = (
        residual_wide * lax.rsqrt(total_sq / D + EPSILON) * ffn_gain.astype(jnp.float32)
    ).astype(jnp.bfloat16)

    fresh_flat = fresh.reshape(row_count, kv_local * channels)
    outgoing = jnp.concatenate([normed_two, fresh_flat], axis=1)
    outgoing_width = outgoing.shape[1]
    received_first, outgoing = lax.optimization_barrier((received_first, outgoing))
    gathered = lax.all_to_all(
        jnp.broadcast_to(outgoing[None], (devices_req,) + outgoing.shape),
        "req",
        split_axis=0,
        concat_axis=0,
        tiled=True,
    ).reshape(total_rows, outgoing_width)
    gathered, parcels_second = lax.optimization_barrier((gathered, parcels_second))
    received_second = lax.all_to_all(
        parcels_second, "req", split_axis=0, concat_axis=0, tiled=True
    )
    lengths_new = lengths[arriving]
    span_first = jnp.where(
        jnp.arange(first_span, dtype=jnp.int32)[None, :, None] < lengths_new[:, None, None],
        received_first[source_owner],
        jnp.zeros((), jnp.bfloat16),
    )
    span_first = jnp.concatenate(
        [span_first, jnp.zeros((row_count, second_span, channels), jnp.bfloat16)], axis=1
    )
    span_first, received_second = lax.optimization_barrier((span_first, received_second))
    normed_all = gathered[:, :width_local]
    fresh_all = gathered[:, width_local:].reshape(total_rows, kv_local, channels)
    ffn_width = w_gate.shape[1]
    joined = jnp.concatenate([w_gate, w_up], axis=1)
    partial_both = jnp.dot(normed_all, joined, preferred_element_type=jnp.float32)
    group_rows = total_rows // devices_kvh
    current = partial_both.reshape(devices_kvh, group_rows, 2 * ffn_width)
    step = devices_kvh // 2
    while step >= 1:
        upper = (kvh_index // step) % 2 == 1
        half = current.shape[0] // 2
        low, high = current[:half], current[half:]
        keep = jnp.where(upper, high, low)
        send = jnp.where(upper, low, high)
        current = keep + lax.ppermute(
            send, "kvh", [(i, i ^ step) for i in range(devices_kvh)]
        )
        step //= 2
    summed = current[0]
    hidden_part = (jax.nn.silu(summed[:, :ffn_width]) * summed[:, ffn_width:]).astype(
        jnp.bfloat16
    )
    block = hidden_part[None]
    step = 1
    while step < devices_kvh:
        upper = (kvh_index // step) % 2 == 1
        other = lax.ppermute(block, "kvh", [(i, i ^ step) for i in range(devices_kvh)])
        block = jnp.where(
            upper, jnp.concatenate([other, block]), jnp.concatenate([block, other])
        )
        step *= 2
    hidden = block.reshape(total_rows, ffn_width)
    lowered_parts = jnp.dot(hidden, w_down, preferred_element_type=jnp.float32)
    lowered_parts, _ = lax.optimization_barrier((lowered_parts, received_second))
    lowered = jnp.sum(
        lax.all_to_all(
            lowered_parts.reshape(devices_req, row_count, width_local),
            "req",
            split_axis=0,
            concat_axis=0,
            tiled=True,
        ),
        axis=0,
    )
    result = (residual_wide + lowered).astype(jnp.bfloat16)

    new_seq = span_first
    second_positions = first_span + jnp.arange(second_span, dtype=jnp.int32)[:, None]
    for slot in range(row_count):
        piece = jnp.where(
            second_positions < lengths_new[slot],
            lax.dynamic_index_in_dim(received_second, source_owner[slot], axis=0, keepdims=False),
            jnp.zeros((), jnp.bfloat16),
        )
        new_seq = lax.dynamic_update_slice(new_seq, piece[None], (slot, first_span, 0))
    new_seq = new_seq.at[jnp.arange(row_count), lengths_new].set(
        fresh_all[arriving].reshape(row_count, channels)
    )
    new_pool = new_seq.reshape(row_count * pages_per, kv_local, page_len, channels)
    return (result, new_pool)


def solution(mesh):
    in_specs = (
        P("req", "kvh"),
        P(),
        P(None, "kvh"),
        P(None, "kvh"),
        P(None, "kvh"),
        P(),
        P(),
        P("kvh", None),
        P("kvh"),
        P("kvh", "req"),
        P("kvh", "req"),
        P("req", "kvh"),
        P("req", "kvh", None, None),
        P(),
        P("req", None),
        P(),
    )
    out_specs = (P("req", "kvh"), P("req", "kvh", None, None))
    return jax.shard_map(
        per_device, mesh=mesh, in_specs=in_specs, out_specs=out_specs, check_vma=False
    )
```

```python
import math

import jax
import jax.numpy as jnp
from jax import lax
from jax.sharding import PartitionSpec as P

D = 2560


EPSILON = 1e-06


def rms_norm(values, norm_gain):
    mean_sq = jnp.mean(values * values, axis=-1, keepdims=True)
    return values * lax.rsqrt(mean_sq + EPSILON) * norm_gain


def rotary(values, positions):
    half_dim = values.shape[-1] // 2
    frequency = jnp.exp(
        jnp.arange(half_dim, dtype=jnp.float32) * (-2.0 * math.log(1000000.0) / values.shape[-1])
    )
    angles = positions.astype(jnp.float32)[:, None, None] * frequency
    cosine = jnp.cos(angles)
    sine_part = jnp.sin(angles)
    first_half = values[..., :half_dim]
    second_half = values[..., half_dim:]
    return jnp.concatenate(
        [
            first_half * cosine - second_half * sine_part,
            second_half * cosine + first_half * sine_part,
        ],
        axis=-1,
    )


def mask_blocks(blocks, lengths_now, fresh, first_page=0):
    row_count, pages_per, kv_local, page_len, channels = blocks.shape
    positions = (
        (first_page + jnp.arange(pages_per, dtype=jnp.int32))[:, None] * page_len
        + jnp.arange(page_len, dtype=jnp.int32)[None, :]
    )
    positions = positions[None, :, None, :, None]
    lengths_col = lengths_now[:, None, None, None, None]
    kept = positions < lengths_col
    placed = positions == lengths_col
    return jnp.where(
        kept,
        blocks,
        jnp.where(placed, fresh[:, None, :, None, :], jnp.zeros((), jnp.bfloat16)),
    )


def attend(query, sequence, lengths_now):
    row_count, kv_local, span_len, channels = sequence.shape
    head_dim = channels // 2
    q_local = query.shape[1]
    group_size = q_local // kv_local
    grouped = query.reshape(row_count, kv_local, group_size, head_dim)
    scores = jnp.einsum(
        "rkgd,rktd->rkgt", grouped, sequence[..., :head_dim], preferred_element_type=jnp.float32
    ) * (1.0 / math.sqrt(head_dim))
    positions = jnp.arange(span_len, dtype=jnp.int32)
    valid = positions[None, None, None, :] <= lengths_now[:, None, None, None]
    scores = jnp.where(valid, scores, -jnp.inf)
    weights = jax.nn.softmax(scores, axis=-1).astype(jnp.bfloat16)
    mixed = jnp.einsum(
        "rkgt,rktd->rkgd", weights, sequence[..., head_dim:], preferred_element_type=jnp.float32
    )
    return mixed.reshape(row_count, q_local * head_dim).astype(jnp.bfloat16)


def per_device(
    states,
    attn_gain,
    w_query,
    w_key,
    w_value,
    query_gain,
    key_gain,
    w_output,
    ffn_gain,
    w_gate,
    w_up,
    w_down,
    kv_pool,
    lengths,
    page_table,
    new_order,
):
    devices_req = lax.axis_size("req")
    my_index = lax.axis_index("req")
    kvh_index = lax.axis_index("kvh")
    row_count = states.shape[0]
    width_local = states.shape[1]
    head_dim = query_gain.shape[0]
    kv_local = w_key.shape[1] // head_dim
    q_local = w_query.shape[1] // head_dim
    pages_per = page_table.shape[1]
    page_len = kv_pool.shape[2]
    channels = 2 * head_dim
    total_rows = new_order.shape[0]

    home = my_index * row_count + jnp.arange(row_count, dtype=jnp.int32)
    new_slot = jnp.sum(
        jnp.where(
            new_order[None, :] == home[:, None],
            jnp.arange(total_rows, dtype=jnp.int32)[None, :],
            0,
        ),
        axis=1,
    )
    destination = new_slot // row_count
    peer_ids = jnp.arange(devices_req, dtype=jnp.int32)
    matches = destination[None, :] == peer_ids[:, None]
    picked_pages = jnp.sum(jnp.where(matches[:, :, None], page_table[None, :, :], 0), axis=1)
    first_pages = pages_per // 2
    second_pages = pages_per - first_pages
    first_span = first_pages * page_len
    parcels_first = kv_pool[picked_pages[:, :first_pages]].reshape(
        devices_req, first_span, channels
    )
    received_first = lax.all_to_all(
        parcels_first, "req", split_axis=0, concat_axis=0, tiled=True
    )
    second_span = second_pages * page_len
    parcels_second = kv_pool[picked_pages[:, first_pages:]].reshape(
        devices_req, second_span, channels
    )
    arriving = lax.dynamic_slice_in_dim(new_order, my_index * row_count, row_count)
    source_owner = arriving // row_count

    full_states = lax.all_gather(states, "kvh", axis=1, tiled=True)
    normed = rms_norm(full_states.astype(jnp.float32), attn_gain.astype(jnp.float32)).astype(
        jnp.bfloat16
    )
    query = jnp.dot(normed, w_query, preferred_element_type=jnp.float32).reshape(
        row_count, q_local, head_dim
    )
    key_new = jnp.dot(normed, w_key, preferred_element_type=jnp.float32).reshape(
        row_count, kv_local, head_dim
    )
    value_new = jnp.dot(normed, w_value, preferred_element_type=jnp.float32).reshape(
        row_count, kv_local, head_dim
    )
    positions_home = lengths[home]
    query = rotary(rms_norm(query, query_gain.astype(jnp.float32)), positions_home).astype(
        jnp.bfloat16
    )
    key_new = rotary(rms_norm(key_new, key_gain.astype(jnp.float32)), positions_home).astype(
        jnp.bfloat16
    )
    fresh = jnp.concatenate([key_new, value_new.astype(jnp.bfloat16)], axis=-1)
    home_blocks = mask_blocks(kv_pool[page_table], positions_home, fresh)
    sequence = home_blocks.transpose(0, 2, 1, 3, 4).reshape(
        row_count, kv_local, pages_per * page_len, channels
    )
    mixed = attend(query, sequence, positions_home)
    partial_out = jnp.dot(mixed, w_output, preferred_element_type=jnp.float32)
    devices_kvh = lax.axis_size("kvh")
    attn_out = partial_out
    step = 1
    while step < devices_kvh:
        attn_out = attn_out + lax.ppermute(
            attn_out, "kvh", [(i, i ^ step) for i in range(devices_kvh)]
        )
        step *= 2
    residual_full = (full_states.astype(jnp.float32) + attn_out).astype(jnp.bfloat16)
    residual_wide_full = residual_full.astype(jnp.float32)
    total_sq = jnp.sum(residual_wide_full * residual_wide_full, axis=-1, keepdims=True)
    residual_wide = lax.dynamic_slice_in_dim(
        residual_wide_full, kvh_index * width_local, width_local, axis=1
    )
    normed_two = (
        residual_wide * lax.rsqrt(total_sq / D + EPSILON) * ffn_gain.astype(jnp.float32)
    ).astype(jnp.bfloat16)

    fresh_flat = fresh.reshape(row_count, kv_local * channels)
    outgoing = jnp.concatenate([normed_two, fresh_flat], axis=1)
    outgoing_width = outgoing.shape[1]
    received_first, outgoing = lax.optimization_barrier((received_first, outgoing))
    gathered = lax.all_to_all(
        jnp.broadcast_to(outgoing[None], (devices_req,) + outgoing.shape),
        "req",
        split_axis=0,
        concat_axis=0,
        tiled=True,
    ).reshape(total_rows, outgoing_width)
    gathered, parcels_second = lax.optimization_barrier((gathered, parcels_second))
    received_second = lax.all_to_all(
        parcels_second, "req", split_axis=0, concat_axis=0, tiled=True
    )
    lengths_new = lengths[arriving]
    span_first = jnp.where(
        jnp.arange(first_span, dtype=jnp.int32)[None, :, None] < lengths_new[:, None, None],
        received_first[source_owner],
        jnp.zeros((), jnp.bfloat16),
    )
    span_first = jnp.concatenate(
        [span_first, jnp.zeros((row_count, second_span, channels), jnp.bfloat16)], axis=1
    )
    span_first, received_second = lax.optimization_barrier((span_first, received_second))
    normed_all = gathered[:, :width_local]
    fresh_all = gathered[:, width_local:].reshape(total_rows, kv_local, channels)
    ffn_width = w_gate.shape[1]
    joined = jnp.concatenate([w_gate, w_up], axis=1)
    partial_both = jnp.dot(normed_all, joined, preferred_element_type=jnp.float32)
    group_rows = total_rows // devices_kvh
    current = partial_both.reshape(devices_kvh, group_rows, 2 * ffn_width)
    step = devices_kvh // 2
    while step >= 1:
        upper = (kvh_index // step) % 2 == 1
        half = current.shape[0] // 2
        low, high = current[:half], current[half:]
        keep = jnp.where(upper, high, low)
        send = jnp.where(upper, low, high)
        current = keep + lax.ppermute(
            send, "kvh", [(i, i ^ step) for i in range(devices_kvh)]
        )
        step //= 2
    summed = current[0]
    hidden_part = (jax.nn.silu(summed[:, :ffn_width]) * summed[:, ffn_width:]).astype(
        jnp.bfloat16
    )
    block = hidden_part[None]
    step = 1
    while step < devices_kvh:
        upper = (kvh_index // step) % 2 == 1
        other = lax.ppermute(block, "kvh", [(i, i ^ step) for i in range(devices_kvh)])
        block = jnp.where(
            upper, jnp.concatenate([other, block]), jnp.concatenate([block, other])
        )
        step *= 2
    hidden = block.reshape(total_rows, ffn_width)
    lowered_parts = jnp.dot(hidden, w_down, preferred_element_type=jnp.float32)
    lowered_parts, _ = lax.optimization_barrier((lowered_parts, received_second))
    lowered = jnp.sum(
        lax.all_to_all(
            lowered_parts.astype(jnp.bfloat16).reshape(devices_req, row_count, width_local),
            "req",
            split_axis=0,
            concat_axis=0,
            tiled=True,
        ).astype(jnp.float32),
        axis=0,
    )
    result = (residual_wide + lowered).astype(jnp.bfloat16)

    new_seq = span_first
    second_positions = first_span + jnp.arange(second_span, dtype=jnp.int32)[:, None]
    for slot in range(row_count):
        piece = jnp.where(
            second_positions < lengths_new[slot],
            lax.dynamic_index_in_dim(received_second, source_owner[slot], axis=0, keepdims=False),
            jnp.zeros((), jnp.bfloat16),
        )
        new_seq = lax.dynamic_update_slice(new_seq, piece[None], (slot, first_span, 0))
    new_seq = new_seq.at[jnp.arange(row_count), lengths_new].set(
        fresh_all[arriving].reshape(row_count, channels)
    )
    new_pool = new_seq.reshape(row_count * pages_per, kv_local, page_len, channels)
    return (result, new_pool)


def solution(mesh):
    in_specs = (
        P("req", "kvh"),
        P(),
        P(None, "kvh"),
        P(None, "kvh"),
        P(None, "kvh"),
        P(),
        P(),
        P("kvh", None),
        P("kvh"),
        P("kvh", "req"),
        P("kvh", "req"),
        P("req", "kvh"),
        P("req", "kvh", None, None),
        P(),
        P("req", None),
        P(),
    )
    out_specs = (P("req", "kvh"), P("req", "kvh", None, None))
    return jax.shard_map(
        per_device, mesh=mesh, in_specs=in_specs, out_specs=out_specs, check_vma=False
    )
```

```python
import math

import jax
import jax.numpy as jnp
from jax import lax
from jax.sharding import PartitionSpec as P

D = 2560


EPSILON = 1e-06


def rms_norm(values, norm_gain):
    mean_sq = jnp.mean(values * values, axis=-1, keepdims=True)
    return values * lax.rsqrt(mean_sq + EPSILON) * norm_gain


def rotary(values, positions):
    half_dim = values.shape[-1] // 2
    frequency = jnp.exp(
        jnp.arange(half_dim, dtype=jnp.float32) * (-2.0 * math.log(1000000.0) / values.shape[-1])
    )
    angles = positions.astype(jnp.float32)[:, None, None] * frequency
    cosine = jnp.cos(angles)
    sine_part = jnp.sin(angles)
    first_half = values[..., :half_dim]
    second_half = values[..., half_dim:]
    return jnp.concatenate(
        [
            first_half * cosine - second_half * sine_part,
            second_half * cosine + first_half * sine_part,
        ],
        axis=-1,
    )


def mask_blocks(blocks, lengths_now, fresh, first_page=0):
    row_count, pages_per, kv_local, page_len, channels = blocks.shape
    positions = (
        (first_page + jnp.arange(pages_per, dtype=jnp.int32))[:, None] * page_len
        + jnp.arange(page_len, dtype=jnp.int32)[None, :]
    )
    positions = positions[None, :, None, :, None]
    lengths_col = lengths_now[:, None, None, None, None]
    kept = positions < lengths_col
    placed = positions == lengths_col
    return jnp.where(
        kept,
        blocks,
        jnp.where(placed, fresh[:, None, :, None, :], jnp.zeros((), jnp.bfloat16)),
    )


def attend(query, sequence, lengths_now):
    row_count, kv_local, span_len, channels = sequence.shape
    head_dim = channels // 2
    q_local = query.shape[1]
    group_size = q_local // kv_local
    grouped = query.reshape(row_count, kv_local, group_size, head_dim)
    scores = jnp.einsum(
        "rkgd,rktd->rkgt", grouped, sequence[..., :head_dim], preferred_element_type=jnp.float32
    ) * (1.0 / math.sqrt(head_dim))
    positions = jnp.arange(span_len, dtype=jnp.int32)
    valid = positions[None, None, None, :] <= lengths_now[:, None, None, None]
    scores = jnp.where(valid, scores, -jnp.inf)
    weights = jax.nn.softmax(scores, axis=-1).astype(jnp.bfloat16)
    mixed = jnp.einsum(
        "rkgt,rktd->rkgd", weights, sequence[..., head_dim:], preferred_element_type=jnp.float32
    )
    return mixed.reshape(row_count, q_local * head_dim).astype(jnp.bfloat16)


def per_device(
    states,
    attn_gain,
    w_query,
    w_key,
    w_value,
    query_gain,
    key_gain,
    w_output,
    ffn_gain,
    w_gate,
    w_up,
    w_down,
    kv_pool,
    lengths,
    page_table,
    new_order,
):
    devices_req = lax.axis_size("req")
    my_index = lax.axis_index("req")
    kvh_index = lax.axis_index("kvh")
    row_count = states.shape[0]
    width_local = states.shape[1]
    head_dim = query_gain.shape[0]
    kv_local = w_key.shape[1] // head_dim
    q_local = w_query.shape[1] // head_dim
    pages_per = page_table.shape[1]
    page_len = kv_pool.shape[2]
    channels = 2 * head_dim
    total_rows = new_order.shape[0]

    home = my_index * row_count + jnp.arange(row_count, dtype=jnp.int32)
    new_slot = jnp.sum(
        jnp.where(
            new_order[None, :] == home[:, None],
            jnp.arange(total_rows, dtype=jnp.int32)[None, :],
            0,
        ),
        axis=1,
    )
    destination = new_slot // row_count
    peer_ids = jnp.arange(devices_req, dtype=jnp.int32)
    matches = destination[None, :] == peer_ids[:, None]
    picked_pages = jnp.sum(jnp.where(matches[:, :, None], page_table[None, :, :], 0), axis=1)
    first_pages = (pages_per * 5) // 8
    second_pages = pages_per - first_pages
    first_span = first_pages * page_len
    parcels_first = kv_pool[picked_pages[:, :first_pages]].reshape(
        devices_req, first_span, channels
    )
    received_first = lax.all_to_all(
        parcels_first, "req", split_axis=0, concat_axis=0, tiled=True
    )
    second_span = second_pages * page_len
    parcels_second = kv_pool[picked_pages[:, first_pages:]].reshape(
        devices_req, second_span, channels
    )
    arriving = lax.dynamic_slice_in_dim(new_order, my_index * row_count, row_count)
    source_owner = arriving // row_count

    full_states = lax.all_gather(states, "kvh", axis=1, tiled=True)
    normed = rms_norm(full_states.astype(jnp.float32), attn_gain.astype(jnp.float32)).astype(
        jnp.bfloat16
    )
    query = jnp.dot(normed, w_query, preferred_element_type=jnp.float32).reshape(
        row_count, q_local, head_dim
    )
    key_new = jnp.dot(normed, w_key, preferred_element_type=jnp.float32).reshape(
        row_count, kv_local, head_dim
    )
    value_new = jnp.dot(normed, w_value, preferred_element_type=jnp.float32).reshape(
        row_count, kv_local, head_dim
    )
    positions_home = lengths[home]
    query = rotary(rms_norm(query, query_gain.astype(jnp.float32)), positions_home).astype(
        jnp.bfloat16
    )
    key_new = rotary(rms_norm(key_new, key_gain.astype(jnp.float32)), positions_home).astype(
        jnp.bfloat16
    )
    fresh = jnp.concatenate([key_new, value_new.astype(jnp.bfloat16)], axis=-1)
    home_blocks = mask_blocks(kv_pool[page_table], positions_home, fresh)
    sequence = home_blocks.transpose(0, 2, 1, 3, 4).reshape(
        row_count, kv_local, pages_per * page_len, channels
    )
    mixed = attend(query, sequence, positions_home)
    partial_out = jnp.dot(mixed, w_output, preferred_element_type=jnp.float32)
    devices_kvh = lax.axis_size("kvh")
    attn_out = partial_out
    step = 1
    while step < devices_kvh:
        attn_out = attn_out + lax.ppermute(
            attn_out, "kvh", [(i, i ^ step) for i in range(devices_kvh)]
        )
        step *= 2
    residual_full = (full_states.astype(jnp.float32) + attn_out).astype(jnp.bfloat16)
    residual_wide_full = residual_full.astype(jnp.float32)
    total_sq = jnp.sum(residual_wide_full * residual_wide_full, axis=-1, keepdims=True)
    residual_wide = lax.dynamic_slice_in_dim(
        residual_wide_full, kvh_index * width_local, width_local, axis=1
    )
    normed_two = (
        residual_wide * lax.rsqrt(total_sq / D + EPSILON) * ffn_gain.astype(jnp.float32)
    ).astype(jnp.bfloat16)

    fresh_flat = fresh.reshape(row_count, kv_local * channels)
    outgoing = jnp.concatenate([normed_two, fresh_flat], axis=1)
    outgoing_width = outgoing.shape[1]
    received_first, outgoing = lax.optimization_barrier((received_first, outgoing))
    gathered = lax.all_to_all(
        jnp.broadcast_to(outgoing[None], (devices_req,) + outgoing.shape),
        "req",
        split_axis=0,
        concat_axis=0,
        tiled=True,
    ).reshape(total_rows, outgoing_width)
    gathered, parcels_second = lax.optimization_barrier((gathered, parcels_second))
    received_second = lax.all_to_all(
        parcels_second, "req", split_axis=0, concat_axis=0, tiled=True
    )
    lengths_new = lengths[arriving]
    span_first = jnp.where(
        jnp.arange(first_span, dtype=jnp.int32)[None, :, None] < lengths_new[:, None, None],
        received_first[source_owner],
        jnp.zeros((), jnp.bfloat16),
    )
    span_first = jnp.concatenate(
        [span_first, jnp.zeros((row_count, second_span, channels), jnp.bfloat16)], axis=1
    )
    span_first, received_second = lax.optimization_barrier((span_first, received_second))
    normed_all = gathered[:, :width_local]
    fresh_all = gathered[:, width_local:].reshape(total_rows, kv_local, channels)
    ffn_width = w_gate.shape[1]
    joined = jnp.concatenate([w_gate, w_up], axis=1)
    partial_both = jnp.dot(normed_all, joined, preferred_element_type=jnp.float32)
    group_rows = total_rows // devices_kvh
    current = partial_both.reshape(devices_kvh, group_rows, 2 * ffn_width)
    step = devices_kvh // 2
    while step >= 1:
        upper = (kvh_index // step) % 2 == 1
        half = current.shape[0] // 2
        low, high = current[:half], current[half:]
        keep = jnp.where(upper, high, low)
        send = jnp.where(upper, low, high)
        current = keep + lax.ppermute(
            send, "kvh", [(i, i ^ step) for i in range(devices_kvh)]
        )
        step //= 2
    summed = current[0]
    hidden_part = (jax.nn.silu(summed[:, :ffn_width]) * summed[:, ffn_width:]).astype(
        jnp.bfloat16
    )
    block = hidden_part[None]
    step = 1
    while step < devices_kvh:
        upper = (kvh_index // step) % 2 == 1
        other = lax.ppermute(block, "kvh", [(i, i ^ step) for i in range(devices_kvh)])
        block = jnp.where(
            upper, jnp.concatenate([other, block]), jnp.concatenate([block, other])
        )
        step *= 2
    hidden = block.reshape(total_rows, ffn_width)
    lowered_parts = jnp.dot(hidden, w_down, preferred_element_type=jnp.float32)
    lowered_parts, _ = lax.optimization_barrier((lowered_parts, received_second))
    lowered = jnp.sum(
        lax.all_to_all(
            lowered_parts.reshape(devices_req, row_count, width_local),
            "req",
            split_axis=0,
            concat_axis=0,
            tiled=True,
        ),
        axis=0,
    )
    result = (residual_wide + lowered).astype(jnp.bfloat16)

    new_seq = span_first
    second_positions = first_span + jnp.arange(second_span, dtype=jnp.int32)[:, None]
    for slot in range(row_count):
        piece = jnp.where(
            second_positions < lengths_new[slot],
            lax.dynamic_index_in_dim(received_second, source_owner[slot], axis=0, keepdims=False),
            jnp.zeros((), jnp.bfloat16),
        )
        new_seq = lax.dynamic_update_slice(new_seq, piece[None], (slot, first_span, 0))
    new_seq = new_seq.at[jnp.arange(row_count), lengths_new].set(
        fresh_all[arriving].reshape(row_count, channels)
    )
    new_pool = new_seq.reshape(row_count * pages_per, kv_local, page_len, channels)
    return (result, new_pool)


def solution(mesh):
    in_specs = (
        P("req", "kvh"),
        P(),
        P(None, "kvh"),
        P(None, "kvh"),
        P(None, "kvh"),
        P(),
        P(),
        P("kvh", None),
        P("kvh"),
        P("kvh", "req"),
        P("kvh", "req"),
        P("req", "kvh"),
        P("req", "kvh", None, None),
        P(),
        P("req", None),
        P(),
    )
    out_specs = (P("req", "kvh"), P("req", "kvh", None, None))
    return jax.shard_map(
        per_device, mesh=mesh, in_specs=in_specs, out_specs=out_specs, check_vma=False
    )
```

```python
import math

import jax
import jax.numpy as jnp
from jax import lax
from jax.sharding import PartitionSpec as P

D = 2560


EPSILON = 1e-06


def rms_norm(values, norm_gain):
    mean_sq = jnp.mean(values * values, axis=-1, keepdims=True)
    return values * lax.rsqrt(mean_sq + EPSILON) * norm_gain


def rotary(values, positions):
    half_dim = values.shape[-1] // 2
    frequency = jnp.exp(
        jnp.arange(half_dim, dtype=jnp.float32) * (-2.0 * math.log(1000000.0) / values.shape[-1])
    )
    angles = positions.astype(jnp.float32)[:, None, None] * frequency
    cosine = jnp.cos(angles)
    sine_part = jnp.sin(angles)
    first_half = values[..., :half_dim]
    second_half = values[..., half_dim:]
    return jnp.concatenate(
        [
            first_half * cosine - second_half * sine_part,
            second_half * cosine + first_half * sine_part,
        ],
        axis=-1,
    )


def mask_blocks(blocks, lengths_now, fresh, first_page=0):
    row_count, pages_per, kv_local, page_len, channels = blocks.shape
    positions = (
        (first_page + jnp.arange(pages_per, dtype=jnp.int32))[:, None] * page_len
        + jnp.arange(page_len, dtype=jnp.int32)[None, :]
    )
    positions = positions[None, :, None, :, None]
    lengths_col = lengths_now[:, None, None, None, None]
    kept = positions < lengths_col
    placed = positions == lengths_col
    return jnp.where(
        kept,
        blocks,
        jnp.where(placed, fresh[:, None, :, None, :], jnp.zeros((), jnp.bfloat16)),
    )


def attend(query, sequence, lengths_now):
    row_count, kv_local, span_len, channels = sequence.shape
    head_dim = channels // 2
    q_local = query.shape[1]
    group_size = q_local // kv_local
    grouped = query.reshape(row_count, kv_local, group_size, head_dim)
    scores = jnp.einsum(
        "rkgd,rktd->rkgt", grouped, sequence[..., :head_dim], preferred_element_type=jnp.float32
    ) * (1.0 / math.sqrt(head_dim))
    positions = jnp.arange(span_len, dtype=jnp.int32)
    valid = positions[None, None, None, :] <= lengths_now[:, None, None, None]
    scores = jnp.where(valid, scores, -jnp.inf)
    weights = jax.nn.softmax(scores, axis=-1).astype(jnp.bfloat16)
    mixed = jnp.einsum(
        "rkgt,rktd->rkgd", weights, sequence[..., head_dim:], preferred_element_type=jnp.float32
    )
    return mixed.reshape(row_count, q_local * head_dim).astype(jnp.bfloat16)


def per_device(
    states,
    attn_gain,
    w_query,
    w_key,
    w_value,
    query_gain,
    key_gain,
    w_output,
    ffn_gain,
    w_gate,
    w_up,
    w_down,
    kv_pool,
    lengths,
    page_table,
    new_order,
):
    devices_req = lax.axis_size("req")
    my_index = lax.axis_index("req")
    kvh_index = lax.axis_index("kvh")
    row_count = states.shape[0]
    width_local = states.shape[1]
    head_dim = query_gain.shape[0]
    kv_local = w_key.shape[1] // head_dim
    q_local = w_query.shape[1] // head_dim
    pages_per = page_table.shape[1]
    page_len = kv_pool.shape[2]
    channels = 2 * head_dim
    total_rows = new_order.shape[0]

    home = my_index * row_count + jnp.arange(row_count, dtype=jnp.int32)
    new_slot = jnp.sum(
        jnp.where(
            new_order[None, :] == home[:, None],
            jnp.arange(total_rows, dtype=jnp.int32)[None, :],
            0,
        ),
        axis=1,
    )
    destination = new_slot // row_count
    peer_ids = jnp.arange(devices_req, dtype=jnp.int32)
    matches = destination[None, :] == peer_ids[:, None]
    picked_pages = jnp.sum(jnp.where(matches[:, :, None], page_table[None, :, :], 0), axis=1)
    first_pages = (pages_per * 3) // 8
    second_pages = pages_per - first_pages
    first_span = first_pages * page_len
    parcels_first = kv_pool[picked_pages[:, :first_pages]].reshape(
        devices_req, first_span, channels
    )
    received_first = lax.all_to_all(
        parcels_first, "req", split_axis=0, concat_axis=0, tiled=True
    )
    second_span = second_pages * page_len
    parcels_second = kv_pool[picked_pages[:, first_pages:]].reshape(
        devices_req, second_span, channels
    )
    arriving = lax.dynamic_slice_in_dim(new_order, my_index * row_count, row_count)
    source_owner = arriving // row_count

    full_states = lax.all_gather(states, "kvh", axis=1, tiled=True)
    normed = rms_norm(full_states.astype(jnp.float32), attn_gain.astype(jnp.float32)).astype(
        jnp.bfloat16
    )
    query = jnp.dot(normed, w_query, preferred_element_type=jnp.float32).reshape(
        row_count, q_local, head_dim
    )
    key_new = jnp.dot(normed, w_key, preferred_element_type=jnp.float32).reshape(
        row_count, kv_local, head_dim
    )
    value_new = jnp.dot(normed, w_value, preferred_element_type=jnp.float32).reshape(
        row_count, kv_local, head_dim
    )
    positions_home = lengths[home]
    query = rotary(rms_norm(query, query_gain.astype(jnp.float32)), positions_home).astype(
        jnp.bfloat16
    )
    key_new = rotary(rms_norm(key_new, key_gain.astype(jnp.float32)), positions_home).astype(
        jnp.bfloat16
    )
    fresh = jnp.concatenate([key_new, value_new.astype(jnp.bfloat16)], axis=-1)
    home_blocks = mask_blocks(kv_pool[page_table], positions_home, fresh)
    sequence = home_blocks.transpose(0, 2, 1, 3, 4).reshape(
        row_count, kv_local, pages_per * page_len, channels
    )
    mixed = attend(query, sequence, positions_home)
    partial_out = jnp.dot(mixed, w_output, preferred_element_type=jnp.float32)
    devices_kvh = lax.axis_size("kvh")
    attn_out = partial_out
    step = 1
    while step < devices_kvh:
        attn_out = attn_out + lax.ppermute(
            attn_out, "kvh", [(i, i ^ step) for i in range(devices_kvh)]
        )
        step *= 2
    residual_full = (full_states.astype(jnp.float32) + attn_out).astype(jnp.bfloat16)
    residual_wide_full = residual_full.astype(jnp.float32)
    total_sq = jnp.sum(residual_wide_full * residual_wide_full, axis=-1, keepdims=True)
    residual_wide = lax.dynamic_slice_in_dim(
        residual_wide_full, kvh_index * width_local, width_local, axis=1
    )
    normed_two = (
        residual_wide * lax.rsqrt(total_sq / D + EPSILON) * ffn_gain.astype(jnp.float32)
    ).astype(jnp.bfloat16)

    fresh_flat = fresh.reshape(row_count, kv_local * channels)
    outgoing = jnp.concatenate([normed_two, fresh_flat], axis=1)
    outgoing_width = outgoing.shape[1]
    received_first, outgoing = lax.optimization_barrier((received_first, outgoing))
    gathered = lax.all_to_all(
        jnp.broadcast_to(outgoing[None], (devices_req,) + outgoing.shape),
        "req",
        split_axis=0,
        concat_axis=0,
        tiled=True,
    ).reshape(total_rows, outgoing_width)
    gathered, parcels_second = lax.optimization_barrier((gathered, parcels_second))
    received_second = lax.all_to_all(
        parcels_second, "req", split_axis=0, concat_axis=0, tiled=True
    )
    lengths_new = lengths[arriving]
    span_first = jnp.where(
        jnp.arange(first_span, dtype=jnp.int32)[None, :, None] < lengths_new[:, None, None],
        received_first[source_owner],
        jnp.zeros((), jnp.bfloat16),
    )
    span_first = jnp.concatenate(
        [span_first, jnp.zeros((row_count, second_span, channels), jnp.bfloat16)], axis=1
    )
    span_first, received_second = lax.optimization_barrier((span_first, received_second))
    normed_all = gathered[:, :width_local]
    fresh_all = gathered[:, width_local:].reshape(total_rows, kv_local, channels)
    ffn_width = w_gate.shape[1]
    joined = jnp.concatenate([w_gate, w_up], axis=1)
    partial_both = jnp.dot(normed_all, joined, preferred_element_type=jnp.float32)
    group_rows = total_rows // devices_kvh
    current = partial_both.reshape(devices_kvh, group_rows, 2 * ffn_width)
    step = devices_kvh // 2
    while step >= 1:
        upper = (kvh_index // step) % 2 == 1
        half = current.shape[0] // 2
        low, high = current[:half], current[half:]
        keep = jnp.where(upper, high, low)
        send = jnp.where(upper, low, high)
        current = keep + lax.ppermute(
            send, "kvh", [(i, i ^ step) for i in range(devices_kvh)]
        )
        step //= 2
    summed = current[0]
    hidden_part = (jax.nn.silu(summed[:, :ffn_width]) * summed[:, ffn_width:]).astype(
        jnp.bfloat16
    )
    block = hidden_part[None]
    step = 1
    while step < devices_kvh:
        upper = (kvh_index // step) % 2 == 1
        other = lax.ppermute(block, "kvh", [(i, i ^ step) for i in range(devices_kvh)])
        block = jnp.where(
            upper, jnp.concatenate([other, block]), jnp.concatenate([block, other])
        )
        step *= 2
    hidden = block.reshape(total_rows, ffn_width)
    lowered_parts = jnp.dot(hidden, w_down, preferred_element_type=jnp.float32)
    lowered_parts, _ = lax.optimization_barrier((lowered_parts, received_second))
    lowered = jnp.sum(
        lax.all_to_all(
            lowered_parts.reshape(devices_req, row_count, width_local),
            "req",
            split_axis=0,
            concat_axis=0,
            tiled=True,
        ),
        axis=0,
    )
    result = (residual_wide + lowered).astype(jnp.bfloat16)

    new_seq = span_first
    second_positions = first_span + jnp.arange(second_span, dtype=jnp.int32)[:, None]
    for slot in range(row_count):
        piece = jnp.where(
            second_positions < lengths_new[slot],
            lax.dynamic_index_in_dim(received_second, source_owner[slot], axis=0, keepdims=False),
            jnp.zeros((), jnp.bfloat16),
        )
        new_seq = lax.dynamic_update_slice(new_seq, piece[None], (slot, first_span, 0))
    new_seq = new_seq.at[jnp.arange(row_count), lengths_new].set(
        fresh_all[arriving].reshape(row_count, channels)
    )
    new_pool = new_seq.reshape(row_count * pages_per, kv_local, page_len, channels)
    return (result, new_pool)


def solution(mesh):
    in_specs = (
        P("req", "kvh"),
        P(),
        P(None, "kvh"),
        P(None, "kvh"),
        P(None, "kvh"),
        P(),
        P(),
        P("kvh", None),
        P("kvh"),
        P("kvh", "req"),
        P("kvh", "req"),
        P("req", "kvh"),
        P("req", "kvh", None, None),
        P(),
        P("req", None),
        P(),
    )
    out_specs = (P("req", "kvh"), P("req", "kvh", None, None))
    return jax.shard_map(
        per_device, mesh=mesh, in_specs=in_specs, out_specs=out_specs, check_vma=False
    )
```
